32 devices in a mesh: groups: 1, gx: 4 (over z), gy: 4 (over y, x), gz: 2 (over core).
Axes of the slice: x: 2, y: 2, z: 4, core: 2. Of those that a mesh axis runs over, the one named last changes fastest.
Arguments:
- modes: float32 [3, 16, 32, 8, 128], P('groups', 'gx', 'gy', 'gz'), may hold values from -6 to 6
- cell_weight: float32 [16, 32, 8], P('gx', 'gy', 'gz'), may hold values from 0.25 to 4
- pair_owner: int32 [32], replicated, may hold values from 0 to 31, each once
Outputs:
- convective: float32 [64, 8256], P('groups', ('gx', 'gy', 'gz'))
The draws below stay inside these ranges and needn't reach their ends.
All inputs are finite; a program needn't handle non-finite values.
Results may differ from the reference program's by a relative error of at most 0.000098.
Values sent between devices are 32-bit elements; how exact they have to be, the bound alone decides.
No kernel may reach another device: no remote copies, remote signals or barrier semaphores. Data moves between devices by JAX's collectives and lax.ppermute only.
A program may use at most 64 MiB of HBM per device.

```python
import math
import jax
import jax.numpy as jnp
import numpy as np
from jax import lax

MODES = 128
TEST = 64
NX = 16
NY = 32
NZ = 8
NOWN = 32
PAIRS = 8256
PBLK = 258
PAIRS_PAD = 8256


def levels(own_key, shape, shards, least, largest):
    def one(dim, parts):
        heights = jax.random.uniform(jax.random.fold_in(jax.random.fold_in(own_key, 6), dim), (parts,), jnp.float32, least / len(shards), largest / len(shards))
        return jnp.repeat(jnp.exp(heights), shape[dim] // parts).reshape((-1,) + (1,) * (len(shape) - dim - 1))

    factor_of = one(*shards[0])
    for cut in shards[1:]:
        factor_of = factor_of * one(*cut)
    return factor_of


def bell_draw(stream_key, shape, deviation, reach, shards=(), kind=jnp.bfloat16):
    values = deviation * jax.random.normal(stream_key, shape, jnp.float32)
    if shards:
        values = values * levels(stream_key, shape, shards, -0.22, 0.18)
    return jnp.clip(values, -reach, reach).astype(kind)


def setup_inputs(seed: int = 0, part: int = 0) -> dict:
    splits = jax.random.split(jax.random.key(seed), 4)
    part_splits = jax.random.split(jax.random.fold_in(splits[3], part), 4)
    return {
        "modes": bell_draw(part_splits[0], (3, NX, NY, NZ, MODES), 1.0, 6.0, ((1, 4), (2, 4), (3, 2)), jnp.float32),
        "cell_weight": jnp.clip(jnp.exp(math.log(4.0) - 2.7725887 * jax.random.uniform(splits[1], (NX, NY, NZ), jnp.float32) ** levels(splits[1], (NX, NY, NZ), ((0, 4), (1, 4), (2, 2)), -0.2, 0.2)), 0.25, 4.0),
        "pair_owner": jax.random.permutation(splits[2], NOWN).astype(jnp.int32),
    }


def gradients(padded):
    step_x = (padded[:, 2:, 1:-1, 1:-1] - padded[:, :-2, 1:-1, 1:-1]) * 0.5
    step_y = (padded[:, 1:-1, 2:, 1:-1] - padded[:, 1:-1, :-2, 1:-1]) * 0.5
    step_z = (padded[:, 1:-1, 1:-1, 2:] - padded[:, 1:-1, 1:-1, :-2]) * 0.5
    return jnp.stack([step_x, step_y, step_z], axis=1)

def assemble(mode_flat, grad_flat, weight_flat, test_count, block_size):
    weighted = mode_flat[:, :, :test_count] * weight_flat[None, :, None]
    cells = weighted.shape[1]
    blocks = weighted.reshape(3, cells, test_count // block_size, block_size).transpose(2, 0, 1, 3)

    def one_block(chosen):
        zeta = jnp.einsum('axi,abxk->ibxk', chosen, grad_flat, precision=lax.Precision.HIGHEST)
        return jnp.einsum('ibxk,bxj->ijk', zeta, mode_flat, precision=lax.Precision.HIGHEST)
    result = lax.map(one_block, blocks)
    width = mode_flat.shape[2]
    return result.reshape(test_count, width, width)

def reference(modes, cell_weight, pair_owner):
    wrapped = jnp.pad(modes, ((0, 0), (1, 1), (1, 1), (0, 0), (0, 0)), mode='wrap')
    padded = jnp.pad(wrapped, ((0, 0), (0, 0), (0, 0), (1, 1), (0, 0)))
    grads = gradients(padded)
    mode_flat = modes.reshape(3, -1, MODES)
    grad_flat = grads.reshape(3, 3, -1, MODES)
    weight_flat = cell_weight.reshape(-1)
    scale = 1.0 / jnp.sqrt(jnp.float32(3.0 * NX * NY * NZ))
    tensor = assemble(mode_flat, grad_flat, weight_flat, TEST, 1) * scale
    upper_j, upper_k = np.triu_indices(MODES)
    table_j = jnp.asarray(upper_j.astype(np.int32))
    table_k = jnp.asarray(upper_k.astype(np.int32))
    slots = jnp.arange(PAIRS_PAD, dtype=jnp.int32)
    owner_slot = slots // PBLK
    within = slots % PBLK
    pair_index = jnp.take(pair_owner, owner_slot) * PBLK + within
    valid = pair_index < PAIRS
    clipped = jnp.minimum(pair_index, PAIRS - 1)
    index_j = jnp.take(table_j, clipped)
    index_k = jnp.take(table_k, clipped)
    flattened = tensor.reshape(TEST, MODES * MODES)
    summed = jnp.take(flattened, index_j * MODES + index_k, axis=1) + jnp.take(flattened, index_k * MODES + index_j, axis=1)
    return jnp.where(valid[None, :], summed, jnp.float32(0.0))
```

```python
import jax
import jax.numpy as jnp
import numpy as np
from jax import lax
from jax.sharding import PartitionSpec as P

TEST = 64


def extended(value, sides, width):
    for axis, dim in sides:
        peers, length = (lax.axis_size(axis), value.shape[dim])
        up = [(i, (i + 1) % peers) for i in range(peers)]
        down = [(j, i) for i, j in up]
        last = lax.slice_in_dim(value, length - width, length, axis=dim)
        leading = lax.slice_in_dim(value, 0, width, axis=dim)
        before = lax.ppermute(last, axis, up)
        after = lax.ppermute(leading, axis, down)
        value = jnp.concatenate([before, value, after], axis=dim)
    return value


def gradients(padded):
    step_x = (padded[:, 2:, 1:-1, 1:-1] - padded[:, :-2, 1:-1, 1:-1]) * 0.5
    step_y = (padded[:, 1:-1, 2:, 1:-1] - padded[:, 1:-1, :-2, 1:-1]) * 0.5
    step_z = (padded[:, 1:-1, 1:-1, 2:] - padded[:, 1:-1, 1:-1, :-2]) * 0.5
    return jnp.stack([step_x, step_y, step_z], axis=1)


def shards(modes, cell_weight, pair_owner):
    width = modes.shape[4]
    size_x = lax.axis_size("gx")
    size_y = lax.axis_size("gy")
    size_z = lax.axis_size("gz")
    owners = size_x * size_y * size_z
    padded = extended(modes, (("gx", 1), ("gy", 2), ("gz", 3)), 1)
    depth = padded.shape[3]
    layer = lax.broadcasted_iota(jnp.int32, (1, 1, 1, depth, 1), 3)
    level = lax.axis_index("gz")
    outside = (layer == 0) & (level == 0) | (layer == depth - 1) & (level == size_z - 1)
    padded = jnp.where(outside, jnp.float32(0.0), padded)
    grads = gradients(padded)
    mode_flat = modes.reshape(3, -1, width)
    grad_flat = grads.reshape(3, 3, -1, width)
    weight_flat = cell_weight.reshape(-1)
    total_cells = modes.shape[1] * modes.shape[2] * modes.shape[3] * owners
    scale = 1.0 / jnp.sqrt(jnp.float32(3.0 * total_cells))
    weighted = mode_flat[:, :, :TEST] * weight_flat[None, :, None]
    zeta = jnp.einsum("axi,abxk->ibxk", weighted, grad_flat, precision=lax.Precision.HIGHEST)
    tensor = jnp.einsum("ibxk,bxj->ijk", zeta, mode_flat, precision=lax.Precision.HIGHEST)
    sym = (tensor + jnp.swapaxes(tensor, 1, 2)) * scale
    pair_total = width * (width + 1) // 2
    block_len = (pair_total + owners - 1) // owners
    rows = [sym[:, j, j:] for j in range(width)]
    slack = block_len * owners - pair_total
    if slack:
        rows.append(jnp.zeros((TEST, slack), jnp.float32))
    canon = jnp.concatenate(rows, axis=1)
    blocks = canon.reshape(TEST, owners, block_len).transpose(1, 0, 2)
    partial_terms = jnp.take(blocks, pair_owner, axis=0)
    owned = lax.psum_scatter(partial_terms, ("gx", "gy", "gz"), scatter_dimension=0, tiled=True)
    return owned.reshape(TEST, block_len)


def solution(mesh):
    placed = (P("groups", "gx", "gy", "gz", None), P("gx", "gy", "gz"), P())
    return jax.shard_map(
        shards,
        mesh=mesh,
        in_specs=placed,
        out_specs=P("groups", ("gx", "gy", "gz")),
        check_vma=False,
    )
```

```python
import jax
import jax.numpy as jnp
import numpy as np
from jax import lax
from jax.sharding import PartitionSpec as P

TEST = 64


def extended(value, sides, width):
    for axis, dim in sides:
        peers, length = (lax.axis_size(axis), value.shape[dim])
        up = [(i, (i + 1) % peers) for i in range(peers)]
        down = [(j, i) for i, j in up]
        last = lax.slice_in_dim(value, length - width, length, axis=dim)
        leading = lax.slice_in_dim(value, 0, width, axis=dim)
        before = lax.ppermute(last, axis, up)
        after = lax.ppermute(leading, axis, down)
        value = jnp.concatenate([before, value, after], axis=dim)
    return value


def gradients(padded):
    step_x = (padded[:, 2:, 1:-1, 1:-1] - padded[:, :-2, 1:-1, 1:-1]) * 0.5
    step_y = (padded[:, 1:-1, 2:, 1:-1] - padded[:, 1:-1, :-2, 1:-1]) * 0.5
    step_z = (padded[:, 1:-1, 1:-1, 2:] - padded[:, 1:-1, 1:-1, :-2]) * 0.5
    return jnp.stack([step_x, step_y, step_z], axis=1)


def halving_stages(axes):
    stages = []
    for axis in axes:
        size = lax.axis_size(axis)
        bit = size // 2
        while bit >= 1:
            stages.append((axis, bit, size))
            bit //= 2
    return stages


def halve(value, axis, bit, size, dim):
    pairs = [(i, i ^ bit) for i in range(size)]
    mine = (lax.axis_index(axis) // bit) % 2
    keep = lax.dynamic_index_in_dim(value, mine, dim, keepdims=True)
    other = lax.dynamic_index_in_dim(value, 1 - mine, dim, keepdims=True)
    return keep + lax.ppermute(other, axis, pairs)


def scatter_sum(payload, axes):
    sizes = [lax.axis_size(a) for a in axes]
    if any(s & (s - 1) for s in sizes):
        return lax.psum_scatter(payload, tuple(axes), scatter_dimension=0, tiled=True)
    stages = halving_stages(axes)
    rows, lanes = payload.shape[1], payload.shape[2]
    value = payload.reshape((2,) * len(stages) + (rows, lanes))
    first = [k for k, s in enumerate(stages) if s[0] == axes[-1]]
    for k in first:
        value = halve(value, *stages[k], k)
    rest = [k for k in range(len(stages)) if k not in first]
    count = min(3, len(rest), rows)
    cuts = np.array_split(np.arange(rows), count) if count else [np.arange(rows)]
    parts = []
    for p, cut in enumerate(cuts):
        part = value[..., int(cut[0]) : int(cut[-1]) + 1, :]
        for k in rest[p:] + rest[:p]:
            part = halve(part, *stages[k], k)
        parts.append(part)
    value = jnp.concatenate(parts, axis=-2) if len(parts) > 1 else parts[0]
    return value.reshape(1, rows, lanes)


def shards(modes, cell_weight, pair_owner):
    width = modes.shape[4]
    size_x = lax.axis_size("gx")
    size_y = lax.axis_size("gy")
    size_z = lax.axis_size("gz")
    owners = size_x * size_y * size_z
    padded = extended(modes, (("gx", 1), ("gy", 2), ("gz", 3)), 1)
    depth = padded.shape[3]
    layer = lax.broadcasted_iota(jnp.int32, (1, 1, 1, depth, 1), 3)
    level = lax.axis_index("gz")
    outside = (layer == 0) & (level == 0) | (layer == depth - 1) & (level == size_z - 1)
    padded = jnp.where(outside, jnp.float32(0.0), padded)
    grads = gradients(padded)
    mode_flat = modes.reshape(3, -1, width)
    grad_flat = grads.reshape(3, 3, -1, width)
    weight_flat = cell_weight.reshape(-1)
    total_cells = modes.shape[1] * modes.shape[2] * modes.shape[3] * owners
    scale = 1.0 / jnp.sqrt(jnp.float32(3.0 * total_cells))
    weighted = mode_flat[:, :, :TEST] * weight_flat[None, :, None]
    zeta = jnp.einsum("axi,abxk->ibxk", weighted, grad_flat, precision=lax.Precision.HIGHEST)
    tensor = jnp.einsum("ibxk,bxj->ijk", zeta, mode_flat, precision=lax.Precision.HIGHEST)
    sym = (tensor + jnp.swapaxes(tensor, 1, 2)) * scale
    pair_total = width * (width + 1) // 2
    block_len = (pair_total + owners - 1) // owners
    rows = [sym[:, j, j:] for j in range(width)]
    slack = block_len * owners - pair_total
    if slack:
        rows.append(jnp.zeros((TEST, slack), jnp.float32))
    canon = jnp.concatenate(rows, axis=1)
    blocks = canon.reshape(TEST, owners, block_len).transpose(1, 0, 2)
    partial_terms = jnp.take(blocks, pair_owner, axis=0).reshape(owners, TEST * block_len)
    lanes = 128
    rows = -(-TEST * block_len // lanes)
    partial_terms = jnp.pad(partial_terms, ((0, 0), (0, rows * lanes - TEST * block_len)))
    owned = scatter_sum(partial_terms.reshape(owners, rows, lanes), ("gx", "gy", "gz"))
    return owned.reshape(-1)[: TEST * block_len].reshape(TEST, block_len)


def solution(mesh):
    placed = (P("groups", "gx", "gy", "gz", None), P("gx", "gy", "gz"), P())
    return jax.shard_map(
        shards,
        mesh=mesh,
        in_specs=placed,
        out_specs=P("groups", ("gx", "gy", "gz")),
        check_vma=False,
    )
```

```python
import jax
import jax.numpy as jnp
import numpy as np
from jax import lax
from jax.experimental import pallas as pl
from jax.experimental.pallas import tpu as pltpu
from jax.sharding import PartitionSpec as P

TEST = 64


def extended(value, sides, width):
    for axis, dim in sides:
        peers, length = (lax.axis_size(axis), value.shape[dim])
        up = [(i, (i + 1) % peers) for i in range(peers)]
        down = [(j, i) for i, j in up]
        last = lax.slice_in_dim(value, length - width, length, axis=dim)
        leading = lax.slice_in_dim(value, 0, width, axis=dim)
        before = lax.ppermute(last, axis, up)
        after = lax.ppermute(leading, axis, down)
        value = jnp.concatenate([before, value, after], axis=dim)
    return value


def gradients(padded):
    step_x = (padded[:, 2:, 1:-1, 1:-1] - padded[:, :-2, 1:-1, 1:-1]) * 0.5
    step_y = (padded[:, 1:-1, 2:, 1:-1] - padded[:, 1:-1, :-2, 1:-1]) * 0.5
    step_z = (padded[:, 1:-1, 1:-1, 2:] - padded[:, 1:-1, 1:-1, :-2]) * 0.5
    return jnp.stack([step_x, step_y, step_z], axis=1)


def halving_stages(axes):
    stages = []
    for axis in axes:
        size = lax.axis_size(axis)
        bit = size // 2
        while bit >= 1:
            stages.append((axis, bit, size))
            bit //= 2
    return stages


def halve(value, axis, bit, size, dim):
    pairs = [(i, i ^ bit) for i in range(size)]
    mine = (lax.axis_index(axis) // bit) % 2
    keep = lax.dynamic_index_in_dim(value, mine, dim, keepdims=True)
    other = lax.dynamic_index_in_dim(value, 1 - mine, dim, keepdims=True)
    return keep + lax.ppermute(other, axis, pairs)


def scatter_sum(payload, axes):
    sizes = [lax.axis_size(a) for a in axes]
    if any(s & (s - 1) for s in sizes):
        return lax.psum_scatter(payload, tuple(axes), scatter_dimension=0, tiled=True)
    stages = halving_stages(axes)
    rows, lanes = payload.shape[1], payload.shape[2]
    value = payload.reshape((2,) * len(stages) + (rows, lanes))
    first = [k for k, s in enumerate(stages) if s[0] == axes[-1]]
    for k in first:
        value = halve(value, *stages[k], k)
    rest = [k for k in range(len(stages)) if k not in first]
    count = min(3, len(rest), rows)
    cuts = np.array_split(np.arange(rows), count) if count else [np.arange(rows)]
    parts = []
    for p, cut in enumerate(cuts):
        part = value[..., int(cut[0]) : int(cut[-1]) + 1, :]
        for k in rest[p:] + rest[:p]:
            part = halve(part, *stages[k], k)
        parts.append(part)
    value = jnp.concatenate(parts, axis=-2) if len(parts) > 1 else parts[0]
    return value.reshape(1, rows, lanes)


def triangle_kernel(w_ref, g_ref, m_ref, out_ref, sym_ref):
    test, width = w_ref.shape[1], m_ref.shape[1]
    out_ref[...] = jnp.zeros(out_ref.shape, out_ref.dtype)

    def contract(i, carry):
        zt = w_ref[0, pl.ds(i, 1), :] * g_ref[0]
        zt = zt + w_ref[1, pl.ds(i, 1), :] * g_ref[1]
        zt = zt + w_ref[2, pl.ds(i, 1), :] * g_ref[2]
        part = jnp.dot(zt, m_ref[...], precision=lax.Precision.HIGHEST, preferred_element_type=jnp.float32)
        start = pl.multiple_of(i * width, width)
        sym_ref[pl.ds(start, width), :] = part + part.T
        return carry

    lax.fori_loop(0, test, contract, 0)
    lane = lax.broadcasted_iota(jnp.int32, (test, 128), 1)

    def place(j, carry):
        slab = sym_ref[pl.ds(j, test, stride=width), :]
        offset = j * width - (j * (j - 1)) // 2
        end = offset % 128 + width - j
        rolled = pltpu.roll(slab, (offset - j) % 128, 1)
        first = pl.multiple_of((offset // 128) * 128, 128)
        second = pl.multiple_of(first + 128, 128)
        low = lane >= offset % 128
        out_ref[:, pl.ds(first, 128)] = jnp.where(low & (lane < end), rolled, out_ref[:, pl.ds(first, 128)])
        out_ref[:, pl.ds(second, 128)] = jnp.where(lane < end - 128, rolled, out_ref[:, pl.ds(second, 128)])
        return carry

    lax.fori_loop(0, width, place, 0)


def triangle(weighted, grads, modes_flat, pair_total, slots):
    test, width = weighted.shape[1], modes_flat.shape[1]
    tiles = max(pair_total // 128 + 2, -(-slots // 128))
    return pl.pallas_call(
        triangle_kernel,
        out_shape=jax.ShapeDtypeStruct((test, tiles * 128), jnp.float32),
        in_specs=[pl.BlockSpec(memory_space=pltpu.VMEM)] * 3,
        out_specs=pl.BlockSpec(memory_space=pltpu.VMEM),
        scratch_shapes=[pltpu.VMEM((test * width, width), jnp.float32)],
    )(weighted, grads, modes_flat)


def shards(modes, cell_weight, pair_owner):
    width = modes.shape[4]
    size_x = lax.axis_size("gx")
    size_y = lax.axis_size("gy")
    size_z = lax.axis_size("gz")
    owners = size_x * size_y * size_z
    padded = extended(modes, (("gx", 1), ("gy", 2), ("gz", 3)), 1)
    depth = padded.shape[3]
    layer = lax.broadcasted_iota(jnp.int32, (1, 1, 1, depth, 1), 3)
    level = lax.axis_index("gz")
    outside = (layer == 0) & (level == 0) | (layer == depth - 1) & (level == size_z - 1)
    padded = jnp.where(outside, jnp.float32(0.0), padded)
    grads = gradients(padded)
    mode_flat = modes.reshape(3, -1, width)
    grad_flat = grads.reshape(3, 3, -1, width)
    weight_flat = cell_weight.reshape(-1)
    total_cells = modes.shape[1] * modes.shape[2] * modes.shape[3] * owners
    scale = 1.0 / jnp.sqrt(jnp.float32(3.0 * total_cells))
    cells = mode_flat.shape[1]
    weighted = mode_flat[:, :, :TEST] * (weight_flat * scale)[None, :, None]
    weighted = jnp.tile(jnp.swapaxes(weighted, 1, 2), (1, 1, 3))
    grads_t = grad_flat.transpose(0, 3, 1, 2).reshape(3, width, 3 * cells)
    pair_total = width * (width + 1) // 2
    block_len = (pair_total + owners - 1) // owners
    canon = triangle(weighted, grads_t, mode_flat.reshape(3 * cells, width), pair_total, owners * block_len)[:, : owners * block_len]
    blocks = canon.reshape(TEST, owners, block_len).transpose(1, 0, 2)
    partial_terms = jnp.take(blocks, pair_owner, axis=0, mode="clip").reshape(owners, TEST * block_len)
    lanes = 128
    rows = -(-TEST * block_len // lanes)
    partial_terms = jnp.pad(partial_terms, ((0, 0), (0, rows * lanes - TEST * block_len)))
    owned = scatter_sum(partial_terms.reshape(owners, rows, lanes), ("gx", "gy", "gz"))
    return owned.reshape(-1)[: TEST * block_len].reshape(TEST, block_len)


def solution(mesh):
    placed = (P("groups", "gx", "gy", "gz", None), P("gx", "gy", "gz"), P())
    return jax.shard_map(
        shards,
        mesh=mesh,
        in_specs=placed,
        out_specs=P("groups", ("gx", "gy", "gz")),
        check_vma=False,
    )
```

```python
import jax
import jax.numpy as jnp
import numpy as np
from jax import lax
from jax.experimental import pallas as pl
from jax.experimental.pallas import tpu as pltpu
from jax.sharding import PartitionSpec as P

TEST = 64


def extended(value, sides, width):
    for axis, dim in sides:
        peers, length = (lax.axis_size(axis), value.shape[dim])
        up = [(i, (i + 1) % peers) for i in range(peers)]
        down = [(j, i) for i, j in up]
        last = lax.slice_in_dim(value, length - width, length, axis=dim)
        leading = lax.slice_in_dim(value, 0, width, axis=dim)
        before = lax.ppermute(last, axis, up)
        after = lax.ppermute(leading, axis, down)
        value = jnp.concatenate([before, value, after], axis=dim)
    return value


def gradients(padded):
    step_x = (padded[:, 2:, 1:-1, 1:-1] - padded[:, :-2, 1:-1, 1:-1]) * 0.5
    step_y = (padded[:, 1:-1, 2:, 1:-1] - padded[:, 1:-1, :-2, 1:-1]) * 0.5
    step_z = (padded[:, 1:-1, 1:-1, 2:] - padded[:, 1:-1, 1:-1, :-2]) * 0.5
    return jnp.stack([step_x, step_y, step_z], axis=1)


def halving_stages(axes):
    stages = []
    for axis in axes:
        size = lax.axis_size(axis)
        bit = size // 2
        while bit >= 1:
            stages.append((axis, bit, size))
            bit //= 2
    return stages


def halve(value, axis, bit, size, dim):
    pairs = [(i, i ^ bit) for i in range(size)]
    mine = (lax.axis_index(axis) // bit) % 2
    keep = lax.dynamic_index_in_dim(value, mine, dim, keepdims=True)
    other = lax.dynamic_index_in_dim(value, 1 - mine, dim, keepdims=True)
    return keep + lax.ppermute(other, axis, pairs)


def scatter_sum(payload, axes):
    sizes = [lax.axis_size(a) for a in axes]
    if any(s & (s - 1) for s in sizes):
        return lax.psum_scatter(payload, tuple(axes), scatter_dimension=0, tiled=True)
    stages = halving_stages(axes)
    rows, lanes = payload.shape[1], payload.shape[2]
    value = payload.reshape((2,) * len(stages) + (rows, lanes))
    first = [k for k, s in enumerate(stages) if s[0] == axes[-1]]
    for k in first:
        value = halve(value, *stages[k], k)
    rest = [k for k in range(len(stages)) if k not in first]
    count = min(3, len(rest), rows)
    cuts = np.array_split(np.arange(rows), count) if count else [np.arange(rows)]
    parts = []
    for p, cut in enumerate(cuts):
        part = value[..., int(cut[0]) : int(cut[-1]) + 1, :]
        for k in rest[p:] + rest[:p]:
            part = halve(part, *stages[k], k)
        parts.append(part)
    value = jnp.concatenate(parts, axis=-2) if len(parts) > 1 else parts[0]
    return value.reshape(1, rows, lanes)


def triangle_kernel(w_ref, g_ref, m_ref, out_ref, sym_ref):
    test, width = w_ref.shape[1], m_ref.shape[1]
    group = 4
    out_ref[...] = jnp.zeros(out_ref.shape, out_ref.dtype)

    def contract(step, carry):
        slabs = []
        for u in range(group):
            i = step * group + u
            zt = w_ref[0, pl.ds(i, 1), :] * g_ref[0]
            zt = zt + w_ref[1, pl.ds(i, 1), :] * g_ref[1]
            zt = zt + w_ref[2, pl.ds(i, 1), :] * g_ref[2]
            slabs.append(zt)
        zt = jnp.concatenate(slabs, axis=0)
        part = jnp.dot(zt, m_ref[...], precision=lax.Precision.HIGHEST, preferred_element_type=jnp.float32)
        for u in range(group):
            piece = part[u * width : (u + 1) * width, :]
            start = pl.multiple_of((step * group + u) * width, width)
            sym_ref[pl.ds(start, width), :] = piece + piece.T
        return carry

    lax.fori_loop(0, test // group, contract, 0)
    lane = lax.broadcasted_iota(jnp.int32, (test, 128), 1)

    def place(j, carry):
        slab = sym_ref[pl.ds(j, test, stride=width), :]
        offset = j * width - (j * (j - 1)) // 2
        end = offset % 128 + width - j
        rolled = pltpu.roll(slab, (offset - j) % 128, 1)
        first = pl.multiple_of((offset // 128) * 128, 128)
        second = pl.multiple_of(first + 128, 128)
        low = lane >= offset % 128
        out_ref[:, pl.ds(first, 128)] = jnp.where(low & (lane < end), rolled, out_ref[:, pl.ds(first, 128)])
        out_ref[:, pl.ds(second, 128)] = jnp.where(lane < end - 128, rolled, out_ref[:, pl.ds(second, 128)])
        return carry

    lax.fori_loop(0, width, place, 0)


def triangle(weighted, grads, modes_flat, pair_total, slots):
    test, width = weighted.shape[1], modes_flat.shape[1]
    tiles = max(pair_total // 128 + 2, -(-slots // 128))
    return pl.pallas_call(
        triangle_kernel,
        out_shape=jax.ShapeDtypeStruct((test, tiles * 128), jnp.float32),
        in_specs=[pl.BlockSpec(memory_space=pltpu.VMEM)] * 3,
        out_specs=pl.BlockSpec(memory_space=pltpu.VMEM),
        scratch_shapes=[pltpu.VMEM((test * width, width), jnp.float32)],
    )(weighted, grads, modes_flat)


def shards(modes, cell_weight, pair_owner):
    width = modes.shape[4]
    size_x = lax.axis_size("gx")
    size_y = lax.axis_size("gy")
    size_z = lax.axis_size("gz")
    owners = size_x * size_y * size_z
    padded = extended(modes, (("gx", 1), ("gy", 2), ("gz", 3)), 1)
    depth = padded.shape[3]
    layer = lax.broadcasted_iota(jnp.int32, (1, 1, 1, depth, 1), 3)
    level = lax.axis_index("gz")
    outside = (layer == 0) & (level == 0) | (layer == depth - 1) & (level == size_z - 1)
    padded = jnp.where(outside, jnp.float32(0.0), padded)
    grads = gradients(padded)
    mode_flat = modes.reshape(3, -1, width)
    grad_flat = grads.reshape(3, 3, -1, width)
    weight_flat = cell_weight.reshape(-1)
    total_cells = modes.shape[1] * modes.shape[2] * modes.shape[3] * owners
    scale = 1.0 / jnp.sqrt(jnp.float32(3.0 * total_cells))
    cells = mode_flat.shape[1]
    weighted = mode_flat[:, :, :TEST] * (weight_flat * scale)[None, :, None]
    weighted = jnp.tile(jnp.swapaxes(weighted, 1, 2), (1, 1, 3))
    grads_t = grad_flat.transpose(0, 3, 1, 2).reshape(3, width, 3 * cells)
    pair_total = width * (width + 1) // 2
    block_len = (pair_total + owners - 1) // owners
    canon = triangle(weighted, grads_t, mode_flat.reshape(3 * cells, width), pair_total, owners * block_len)[:, : owners * block_len]
    blocks = canon.reshape(TEST, owners, block_len).transpose(1, 0, 2)
    partial_terms = jnp.take(blocks, pair_owner, axis=0, mode="clip").reshape(owners, TEST * block_len)
    lanes = 128
    rows = -(-TEST * block_len // lanes)
    partial_terms = jnp.pad(partial_terms, ((0, 0), (0, rows * lanes - TEST * block_len)))
    owned = scatter_sum(partial_terms.reshape(owners, rows, lanes), ("gx", "gy", "gz"))
    return owned.reshape(-1)[: TEST * block_len].reshape(TEST, block_len)


def solution(mesh):
    placed = (P("groups", "gx", "gy", "gz", None), P("gx", "gy", "gz"), P())
    return jax.shard_map(
        shards,
        mesh=mesh,
        in_specs=placed,
        out_specs=P("groups", ("gx", "gy", "gz")),
        check_vma=False,
    )
```

```python
import jax
import jax.numpy as jnp
import numpy as np
from jax import lax
from jax.experimental import pallas as pl
from jax.experimental.pallas import tpu as pltpu
from jax.sharding import PartitionSpec as P

TEST = 64


def extended(value, sides, width):
    for axis, dim in sides:
        peers, length = (lax.axis_size(axis), value.shape[dim])
        up = [(i, (i + 1) % peers) for i in range(peers)]
        down = [(j, i) for i, j in up]
        last = lax.slice_in_dim(value, length - width, length, axis=dim)
        leading = lax.slice_in_dim(value, 0, width, axis=dim)
        before = lax.ppermute(last, axis, up)
        after = lax.ppermute(leading, axis, down)
        value = jnp.concatenate([before, value, after], axis=dim)
    return value


def gradients(padded):
    step_x = (padded[:, 2:, 1:-1, 1:-1] - padded[:, :-2, 1:-1, 1:-1]) * 0.5
    step_y = (padded[:, 1:-1, 2:, 1:-1] - padded[:, 1:-1, :-2, 1:-1]) * 0.5
    step_z = (padded[:, 1:-1, 1:-1, 2:] - padded[:, 1:-1, 1:-1, :-2]) * 0.5
    return jnp.stack([step_x, step_y, step_z], axis=1)


def face_gradients(value):
    steps = []
    for axis, dim in (("gx", 1), ("gy", 2), ("gz", 3)):
        peers, length = lax.axis_size(axis), value.shape[dim]
        up = [(i, (i + 1) % peers) for i in range(peers)]
        down = [(j, i) for i, j in up]
        before = lax.ppermute(lax.slice_in_dim(value, length - 1, length, axis=dim), axis, up)
        after = lax.ppermute(lax.slice_in_dim(value, 0, 1, axis=dim), axis, down)
        if axis == "gz":
            level = lax.axis_index(axis)
            before = jnp.where(level == 0, jnp.float32(0.0), before)
            after = jnp.where(level == peers - 1, jnp.float32(0.0), after)
        ext = jnp.concatenate([before, value, after], axis=dim)
        high = lax.slice_in_dim(ext, 2, length + 2, axis=dim)
        low = lax.slice_in_dim(ext, 0, length, axis=dim)
        steps.append((high - low) * 0.5)
    return jnp.stack(steps, axis=1)


def halving_stages(axes):
    stages = []
    for axis in axes:
        size = lax.axis_size(axis)
        bit = size // 2
        while bit >= 1:
            stages.append((axis, bit, size))
            bit //= 2
    return stages


def halve(value, axis, bit, size, dim):
    pairs = [(i, i ^ bit) for i in range(size)]
    mine = (lax.axis_index(axis) // bit) % 2
    keep = lax.dynamic_index_in_dim(value, mine, dim, keepdims=True)
    other = lax.dynamic_index_in_dim(value, 1 - mine, dim, keepdims=True)
    return keep + lax.ppermute(other, axis, pairs)


def scatter_sum(payload, axes):
    sizes = [lax.axis_size(a) for a in axes]
    if any(s & (s - 1) for s in sizes):
        return lax.psum_scatter(payload, tuple(axes), scatter_dimension=0, tiled=True)
    stages = halving_stages(axes)
    rows, lanes = payload.shape[1], payload.shape[2]
    value = payload.reshape((2,) * len(stages) + (rows, lanes))
    first = [k for k, s in enumerate(stages) if s[0] == axes[-1]]
    for k in first:
        value = halve(value, *stages[k], k)
    rest = [k for k in range(len(stages)) if k not in first]
    count = min(3, len(rest), rows)
    cuts = np.array_split(np.arange(rows), count) if count else [np.arange(rows)]
    parts = []
    for p, cut in enumerate(cuts):
        part = value[..., int(cut[0]) : int(cut[-1]) + 1, :]
        for k in rest[p:] + rest[:p]:
            part = halve(part, *stages[k], k)
        parts.append(part)
    value = jnp.concatenate(parts, axis=-2) if len(parts) > 1 else parts[0]
    return value.reshape(1, rows, lanes)


def triangle_kernel(w_ref, g_ref, m_ref, out_ref, sym_ref):
    test, width = w_ref.shape[1], m_ref.shape[1]
    group = 4
    out_ref[...] = jnp.zeros(out_ref.shape, out_ref.dtype)

    def contract(step, carry):
        slabs = []
        for u in range(group):
            i = step * group + u
            zt = w_ref[0, pl.ds(i, 1), :] * g_ref[0]
            zt = zt + w_ref[1, pl.ds(i, 1), :] * g_ref[1]
            zt = zt + w_ref[2, pl.ds(i, 1), :] * g_ref[2]
            slabs.append(zt)
        zt = jnp.concatenate(slabs, axis=0)
        part = jnp.dot(zt, m_ref[...], precision=lax.Precision.HIGHEST, preferred_element_type=jnp.float32)
        for u in range(group):
            piece = part[u * width : (u + 1) * width, :]
            start = pl.multiple_of((step * group + u) * width, width)
            sym_ref[pl.ds(start, width), :] = piece + piece.T
        return carry

    lax.fori_loop(0, test // group, contract, 0)
    lane = lax.broadcasted_iota(jnp.int32, (test, 128), 1)

    def place(j, carry):
        slab = sym_ref[pl.ds(j, test, stride=width), :]
        offset = j * width - (j * (j - 1)) // 2
        end = offset % 128 + width - j
        rolled = pltpu.roll(slab, (offset - j) % 128, 1)
        first = pl.multiple_of((offset // 128) * 128, 128)
        second = pl.multiple_of(first + 128, 128)
        low = lane >= offset % 128
        out_ref[:, pl.ds(first, 128)] = jnp.where(low & (lane < end), rolled, out_ref[:, pl.ds(first, 128)])
        out_ref[:, pl.ds(second, 128)] = jnp.where(lane < end - 128, rolled, out_ref[:, pl.ds(second, 128)])
        return carry

    lax.fori_loop(0, width, place, 0)


def triangle(weighted, grads, modes_flat, pair_total, slots):
    test, width = weighted.shape[1], modes_flat.shape[1]
    tiles = max(pair_total // 128 + 2, -(-slots // 128))
    return pl.pallas_call(
        triangle_kernel,
        out_shape=jax.ShapeDtypeStruct((test, tiles * 128), jnp.float32),
        in_specs=[pl.BlockSpec(memory_space=pltpu.VMEM)] * 3,
        out_specs=pl.BlockSpec(memory_space=pltpu.VMEM),
        scratch_shapes=[pltpu.VMEM((test * width, width), jnp.float32)],
    )(weighted, grads, modes_flat)


def shards(modes, cell_weight, pair_owner):
    width = modes.shape[4]
    size_x = lax.axis_size("gx")
    size_y = lax.axis_size("gy")
    size_z = lax.axis_size("gz")
    owners = size_x * size_y * size_z
    grads = face_gradients(modes)
    mode_flat = modes.reshape(3, -1, width)
    grad_flat = grads.reshape(3, 3, -1, width)
    weight_flat = cell_weight.reshape(-1)
    total_cells = modes.shape[1] * modes.shape[2] * modes.shape[3] * owners
    scale = 1.0 / jnp.sqrt(jnp.float32(3.0 * total_cells))
    cells = mode_flat.shape[1]
    weighted = mode_flat[:, :, :TEST] * (weight_flat * scale)[None, :, None]
    weighted = jnp.tile(jnp.swapaxes(weighted, 1, 2), (1, 1, 3))
    grads_t = grad_flat.transpose(0, 3, 1, 2).reshape(3, width, 3 * cells)
    pair_total = width * (width + 1) // 2
    block_len = (pair_total + owners - 1) // owners
    canon = triangle(weighted, grads_t, mode_flat.reshape(3 * cells, width), pair_total, owners * block_len)[:, : owners * block_len]
    blocks = canon.reshape(TEST, owners, block_len).transpose(1, 0, 2)
    partial_terms = jnp.take(blocks, pair_owner, axis=0, mode="clip").reshape(owners, TEST * block_len)
    lanes = 128
    rows = -(-TEST * block_len // lanes)
    partial_terms = jnp.pad(partial_terms, ((0, 0), (0, rows * lanes - TEST * block_len)))
    owned = scatter_sum(partial_terms.reshape(owners, rows, lanes), ("gx", "gy", "gz"))
    return owned.reshape(-1)[: TEST * block_len].reshape(TEST, block_len)


def solution(mesh):
    placed = (P("groups", "gx", "gy", "gz", None), P("gx", "gy", "gz"), P())
    return jax.shard_map(
        shards,
        mesh=mesh,
        in_specs=placed,
        out_specs=P("groups", ("gx", "gy", "gz")),
        check_vma=False,
    )
```

```python
import functools

import jax
import jax.numpy as jnp
import numpy as np
from jax import lax
from jax.experimental import pallas as pl
from jax.experimental.pallas import tpu as pltpu
from jax.sharding import PartitionSpec as P

TEST = 64


def extended(value, sides, width):
    for axis, dim in sides:
        peers, length = (lax.axis_size(axis), value.shape[dim])
        up = [(i, (i + 1) % peers) for i in range(peers)]
        down = [(j, i) for i, j in up]
        last = lax.slice_in_dim(value, length - width, length, axis=dim)
        leading = lax.slice_in_dim(value, 0, width, axis=dim)
        before = lax.ppermute(last, axis, up)
        after = lax.ppermute(leading, axis, down)
        value = jnp.concatenate([before, value, after], axis=dim)
    return value


def gradients(padded):
    step_x = (padded[:, 2:, 1:-1, 1:-1] - padded[:, :-2, 1:-1, 1:-1]) * 0.5
    step_y = (padded[:, 1:-1, 2:, 1:-1] - padded[:, 1:-1, :-2, 1:-1]) * 0.5
    step_z = (padded[:, 1:-1, 1:-1, 2:] - padded[:, 1:-1, 1:-1, :-2]) * 0.5
    return jnp.stack([step_x, step_y, step_z], axis=1)


def face_gradients(value):
    steps = []
    for axis, dim in (("gx", 1), ("gy", 2), ("gz", 3)):
        peers, length = lax.axis_size(axis), value.shape[dim]
        up = [(i, (i + 1) % peers) for i in range(peers)]
        down = [(j, i) for i, j in up]
        before = lax.ppermute(lax.slice_in_dim(value, length - 1, length, axis=dim), axis, up)
        after = lax.ppermute(lax.slice_in_dim(value, 0, 1, axis=dim), axis, down)
        if axis == "gz":
            level = lax.axis_index(axis)
            before = jnp.where(level == 0, jnp.float32(0.0), before)
            after = jnp.where(level == peers - 1, jnp.float32(0.0), after)
        ext = jnp.concatenate([before, value, after], axis=dim)
        high = lax.slice_in_dim(ext, 2, length + 2, axis=dim)
        low = lax.slice_in_dim(ext, 0, length, axis=dim)
        steps.append((high - low) * 0.5)
    return jnp.stack(steps, axis=1)


def halving_stages(axes):
    stages = []
    for axis in axes:
        size = lax.axis_size(axis)
        bit = size // 2
        while bit >= 1:
            stages.append((axis, bit, size))
            bit //= 2
    return stages


def halve(value, axis, bit, size, dim):
    pairs = [(i, i ^ bit) for i in range(size)]
    mine = (lax.axis_index(axis) // bit) % 2
    keep = lax.dynamic_index_in_dim(value, mine, dim, keepdims=True)
    other = lax.dynamic_index_in_dim(value, 1 - mine, dim, keepdims=True)
    return keep + lax.ppermute(other, axis, pairs)


def scatter_sum(payload, axes):
    sizes = [lax.axis_size(a) for a in axes]
    if any(s & (s - 1) for s in sizes):
        return lax.psum_scatter(payload, tuple(axes), scatter_dimension=0, tiled=True)
    stages = halving_stages(axes)
    rows, lanes = payload.shape[1], payload.shape[2]
    value = payload.reshape((2,) * len(stages) + (rows, lanes))
    first = [k for k, s in enumerate(stages) if s[0] == axes[-1]]
    for k in first:
        value = halve(value, *stages[k], k)
    rest = [k for k in range(len(stages)) if k not in first]
    count = min(3, len(rest), rows)
    cuts = np.array_split(np.arange(rows), count) if count else [np.arange(rows)]
    parts = []
    for p, cut in enumerate(cuts):
        part = value[..., int(cut[0]) : int(cut[-1]) + 1, :]
        for k in rest[p:] + rest[:p]:
            part = halve(part, *stages[k], k)
        parts.append(part)
    value = jnp.concatenate(parts, axis=-2) if len(parts) > 1 else parts[0]
    return value.reshape(1, rows, lanes)


def triangle_kernel(block_len, slot_ref, w_ref, g_ref, m_ref, out_ref, sym_ref):
    test, width = w_ref.shape[1], m_ref.shape[1]
    group = 4
    out_ref[...] = jnp.zeros(out_ref.shape, out_ref.dtype)

    def contract(step, carry):
        slabs = []
        for u in range(group):
            i = step * group + u
            zt = w_ref[0, pl.ds(i, 1), :] * g_ref[0]
            zt = zt + w_ref[1, pl.ds(i, 1), :] * g_ref[1]
            zt = zt + w_ref[2, pl.ds(i, 1), :] * g_ref[2]
            slabs.append(zt)
        zt = jnp.concatenate(slabs, axis=0)
        part = jnp.dot(zt, m_ref[...], precision=lax.Precision.HIGHEST, preferred_element_type=jnp.float32)
        for u in range(group):
            piece = part[u * width : (u + 1) * width, :]
            start = pl.multiple_of((step * group + u) * width, width)
            sym_ref[pl.ds(start, width), :] = piece + piece.T
        return carry

    lax.fori_loop(0, test // group, contract, 0)
    lane = lax.broadcasted_iota(jnp.int32, (test, 128), 1)

    def place(j, carry):
        slab = sym_ref[pl.ds(j, test, stride=width), :]
        offset = j * width - (j * (j - 1)) // 2
        stop = offset + width - j

        def per_block(c, carry):
            base_c = c * block_len
            lo = jnp.maximum(offset, base_c) - base_c
            hi = jnp.minimum(stop, base_c + block_len) - base_c
            slot = slot_ref[c]

            def per_tile(u, carry):
                base = base_c + u * 128
                rolled = pltpu.roll(slab, (offset - j - base) % 128, 1)
                keep = (lane >= lo - u * 128) & (lane < hi - u * 128)
                at = pl.multiple_of(u * 128, 128)
                cur = out_ref[slot, :, pl.ds(at, 128)]
                out_ref[slot, :, pl.ds(at, 128)] = jnp.where(keep, rolled, cur)
                return carry

            return lax.fori_loop(lo // 128, (hi - 1) // 128 + 1, per_tile, carry)

        return lax.fori_loop(offset // block_len, (stop - 1) // block_len + 1, per_block, carry)

    lax.fori_loop(0, width, place, 0)


def triangle(slots, weighted, grads, modes_flat, block_len):
    owners = slots.shape[0]
    test, width = weighted.shape[1], modes_flat.shape[1]
    tiles = -(-block_len // 128)
    return pl.pallas_call(
        functools.partial(triangle_kernel, block_len),
        out_shape=jax.ShapeDtypeStruct((owners, test, tiles * 128), jnp.float32),
        in_specs=[pl.BlockSpec(memory_space=pltpu.SMEM)] + [pl.BlockSpec(memory_space=pltpu.VMEM)] * 3,
        out_specs=pl.BlockSpec(memory_space=pltpu.VMEM),
        scratch_shapes=[pltpu.VMEM((test * width, width), jnp.float32)],
    )(slots, weighted, grads, modes_flat)


def shards(modes, cell_weight, pair_owner):
    width = modes.shape[4]
    size_x = lax.axis_size("gx")
    size_y = lax.axis_size("gy")
    size_z = lax.axis_size("gz")
    owners = size_x * size_y * size_z
    grads = face_gradients(modes)
    mode_flat = modes.reshape(3, -1, width)
    grad_flat = grads.reshape(3, 3, -1, width)
    weight_flat = cell_weight.reshape(-1)
    total_cells = modes.shape[1] * modes.shape[2] * modes.shape[3] * owners
    scale = 1.0 / jnp.sqrt(jnp.float32(3.0 * total_cells))
    cells = mode_flat.shape[1]
    weighted = mode_flat[:, :, :TEST] * (weight_flat * scale)[None, :, None]
    weighted = jnp.tile(jnp.swapaxes(weighted, 1, 2), (1, 1, 3))
    grads_t = grad_flat.transpose(0, 3, 1, 2).reshape(3, width, 3 * cells)
    pair_total = width * (width + 1) // 2
    block_len = (pair_total + owners - 1) // owners
    ranks = jnp.arange(owners, dtype=jnp.int32)
    slots = jnp.sum(jnp.where(pair_owner[None, :] == ranks[:, None], ranks[None, :], 0), axis=1)
    slots = jnp.clip(slots, 0, owners - 1).astype(jnp.int32)
    placed = triangle(slots, weighted, grads_t, mode_flat.reshape(3 * cells, width), block_len)
    partial_terms = placed[:, :, :block_len].reshape(owners, TEST * block_len)
    lanes = 128
    rows = -(-TEST * block_len // lanes)
    partial_terms = jnp.pad(partial_terms, ((0, 0), (0, rows * lanes - TEST * block_len)))
    owned = scatter_sum(partial_terms.reshape(owners, rows, lanes), ("gx", "gy", "gz"))
    return owned.reshape(-1)[: TEST * block_len].reshape(TEST, block_len)


def solution(mesh):
    placed = (P("groups", "gx", "gy", "gz", None), P("gx", "gy", "gz"), P())
    return jax.shard_map(
        shards,
        mesh=mesh,
        in_specs=placed,
        out_specs=P("groups", ("gx", "gy", "gz")),
        check_vma=False,
    )
```

```python
import functools

import jax
import jax.numpy as jnp
import numpy as np
from jax import lax
from jax.experimental import pallas as pl
from jax.experimental.pallas import tpu as pltpu
from jax.sharding import PartitionSpec as P

TEST = 64


def extended(value, sides, width):
    for axis, dim in sides:
        peers, length = (lax.axis_size(axis), value.shape[dim])
        up = [(i, (i + 1) % peers) for i in range(peers)]
        down = [(j, i) for i, j in up]
        last = lax.slice_in_dim(value, length - width, length, axis=dim)
        leading = lax.slice_in_dim(value, 0, width, axis=dim)
        before = lax.ppermute(last, axis, up)
        after = lax.ppermute(leading, axis, down)
        value = jnp.concatenate([before, value, after], axis=dim)
    return value


def gradients(padded):
    step_x = (padded[:, 2:, 1:-1, 1:-1] - padded[:, :-2, 1:-1, 1:-1]) * 0.5
    step_y = (padded[:, 1:-1, 2:, 1:-1] - padded[:, 1:-1, :-2, 1:-1]) * 0.5
    step_z = (padded[:, 1:-1, 1:-1, 2:] - padded[:, 1:-1, 1:-1, :-2]) * 0.5
    return jnp.stack([step_x, step_y, step_z], axis=1)


def face_gradients(value):
    steps = []
    for axis, dim in (("gx", 1), ("gy", 2), ("gz", 3)):
        peers, length = lax.axis_size(axis), value.shape[dim]
        up = [(i, (i + 1) % peers) for i in range(peers)]
        down = [(j, i) for i, j in up]
        before = lax.ppermute(lax.slice_in_dim(value, length - 1, length, axis=dim), axis, up)
        after = lax.ppermute(lax.slice_in_dim(value, 0, 1, axis=dim), axis, down)
        if axis == "gz":
            level = lax.axis_index(axis)
            before = jnp.where(level == 0, jnp.float32(0.0), before)
            after = jnp.where(level == peers - 1, jnp.float32(0.0), after)
        ext = jnp.concatenate([before, value, after], axis=dim)
        high = lax.slice_in_dim(ext, 2, length + 2, axis=dim)
        low = lax.slice_in_dim(ext, 0, length, axis=dim)
        steps.append((high - low) * 0.5)
    return jnp.stack(steps, axis=1)


def halving_stages(axes):
    stages = []
    for axis in axes:
        size = lax.axis_size(axis)
        bit = size // 2
        while bit >= 1:
            stages.append((axis, bit, size))
            bit //= 2
    return stages


def halve(value, axis, bit, size, dim):
    pairs = [(i, i ^ bit) for i in range(size)]
    mine = (lax.axis_index(axis) // bit) % 2
    keep = lax.dynamic_index_in_dim(value, mine, dim, keepdims=True)
    other = lax.dynamic_index_in_dim(value, 1 - mine, dim, keepdims=True)
    return keep + lax.ppermute(other, axis, pairs)


def scatter_sum(payload, axes):
    sizes = [lax.axis_size(a) for a in axes]
    if any(s & (s - 1) for s in sizes):
        return lax.psum_scatter(payload, tuple(axes), scatter_dimension=0, tiled=True)
    stages = halving_stages(axes)
    rows, lanes = payload.shape[1], payload.shape[2]
    value = payload.reshape((2,) * len(stages) + (rows, lanes))
    first = [k for k, s in enumerate(stages) if s[0] == axes[-1]]
    for k in first:
        value = halve(value, *stages[k], k)
    rest = [k for k in range(len(stages)) if k not in first]
    count = min(3, len(rest), rows)
    cuts = np.array_split(np.arange(rows), count) if count else [np.arange(rows)]
    parts = []
    for p, cut in enumerate(cuts):
        part = value[..., int(cut[0]) : int(cut[-1]) + 1, :]
        for k in rest[p:] + rest[:p]:
            part = halve(part, *stages[k], k)
        parts.append(part)
    value = jnp.concatenate(parts, axis=-2) if len(parts) > 1 else parts[0]
    return value.reshape(1, rows, lanes)


def triangle_kernel(block_len, slot_ref, w_ref, g_ref, m_ref, out_ref, sym_ref):
    test, width = w_ref.shape[1], m_ref.shape[1]
    group = 4
    out_ref[...] = jnp.zeros(out_ref.shape, out_ref.dtype)

    def contract(step, carry):
        slabs = []
        for u in range(group):
            i = step * group + u
            zt = w_ref[0, pl.ds(i, 1), :] * g_ref[0]
            zt = zt + w_ref[1, pl.ds(i, 1), :] * g_ref[1]
            zt = zt + w_ref[2, pl.ds(i, 1), :] * g_ref[2]
            slabs.append(zt)
        zt = jnp.concatenate(slabs, axis=0)
        part = jnp.dot(zt, m_ref[...], precision=lax.Precision.HIGHEST, preferred_element_type=jnp.float32)
        for u in range(group):
            piece = part[u * width : (u + 1) * width, :]
            start = pl.multiple_of((step * group + u) * width, width)
            sym_ref[pl.ds(start, width), :] = piece + piece.T
        return carry

    lax.fori_loop(0, test // group, contract, 0)
    lane = lax.broadcasted_iota(jnp.int32, (test, 128), 1)
    for j in range(width):
        slab = sym_ref[pl.ds(j, test, stride=width), :]
        offset = j * width - (j * (j - 1)) // 2
        stop = offset + width - j
        for c in range(offset // block_len, (stop - 1) // block_len + 1):
            lo = max(offset, c * block_len) - c * block_len
            hi = min(stop, (c + 1) * block_len) - c * block_len
            slot = slot_ref[c]
            for u in range(lo // 128, (hi - 1) // 128 + 1):
                base = c * block_len + u * 128
                rolled = pltpu.roll(slab, (offset - j - base) % 128, 1)
                keep = (lane >= lo - u * 128) & (lane < hi - u * 128)
                cur = out_ref[slot, :, pl.ds(u * 128, 128)]
                out_ref[slot, :, pl.ds(u * 128, 128)] = jnp.where(keep, rolled, cur)


def triangle(slots, weighted, grads, modes_flat, block_len):
    owners = slots.shape[0]
    test, width = weighted.shape[1], modes_flat.shape[1]
    tiles = -(-block_len // 128)
    return pl.pallas_call(
        functools.partial(triangle_kernel, block_len),
        out_shape=jax.ShapeDtypeStruct((owners, test, tiles * 128), jnp.float32),
        in_specs=[pl.BlockSpec(memory_space=pltpu.SMEM)] + [pl.BlockSpec(memory_space=pltpu.VMEM)] * 3,
        out_specs=pl.BlockSpec(memory_space=pltpu.VMEM),
        scratch_shapes=[pltpu.VMEM((test * width, width), jnp.float32)],
    )(slots, weighted, grads, modes_flat)


def shards(modes, cell_weight, pair_owner):
    width = modes.shape[4]
    size_x = lax.axis_size("gx")
    size_y = lax.axis_size("gy")
    size_z = lax.axis_size("gz")
    owners = size_x * size_y * size_z
    grads = face_gradients(modes)
    mode_flat = modes.reshape(3, -1, width)
    grad_flat = grads.reshape(3, 3, -1, width)
    weight_flat = cell_weight.reshape(-1)
    total_cells = modes.shape[1] * modes.shape[2] * modes.shape[3] * owners
    scale = 1.0 / jnp.sqrt(jnp.float32(3.0 * total_cells))
    cells = mode_flat.shape[1]
    weighted = mode_flat[:, :, :TEST] * (weight_flat * scale)[None, :, None]
    weighted = jnp.tile(jnp.swapaxes(weighted, 1, 2), (1, 1, 3))
    grads_t = grad_flat.transpose(0, 3, 1, 2).reshape(3, width, 3 * cells)
    pair_total = width * (width + 1) // 2
    block_len = (pair_total + owners - 1) // owners
    ranks = jnp.arange(owners, dtype=jnp.int32)
    slots = jnp.sum(jnp.where(pair_owner[None, :] == ranks[:, None], ranks[None, :], 0), axis=1)
    slots = jnp.clip(slots, 0, owners - 1).astype(jnp.int32)
    placed = triangle(slots, weighted, grads_t, mode_flat.reshape(3 * cells, width), block_len)
    partial_terms = placed[:, :, :block_len].reshape(owners, TEST * block_len)
    lanes = 128
    rows = -(-TEST * block_len // lanes)
    partial_terms = jnp.pad(partial_terms, ((0, 0), (0, rows * lanes - TEST * block_len)))
    owned = scatter_sum(partial_terms.reshape(owners, rows, lanes), ("gx", "gy", "gz"))
    return owned.reshape(-1)[: TEST * block_len].reshape(TEST, block_len)


def solution(mesh):
    placed = (P("groups", "gx", "gy", "gz", None), P("gx", "gy", "gz"), P())
    return jax.shard_map(
        shards,
        mesh=mesh,
        in_specs=placed,
        out_specs=P("groups", ("gx", "gy", "gz")),
        check_vma=False,
    )
```

```python
import functools

import jax
import jax.numpy as jnp
import numpy as np
from jax import lax
from jax.experimental import pallas as pl
from jax.experimental.pallas import tpu as pltpu
from jax.sharding import PartitionSpec as P

TEST = 64


def extended(value, sides, width):
    for axis, dim in sides:
        peers, length = (lax.axis_size(axis), value.shape[dim])
        up = [(i, (i + 1) % peers) for i in range(peers)]
        down = [(j, i) for i, j in up]
        last = lax.slice_in_dim(value, length - width, length, axis=dim)
        leading = lax.slice_in_dim(value, 0, width, axis=dim)
        before = lax.ppermute(last, axis, up)
        after = lax.ppermute(leading, axis, down)
        value = jnp.concatenate([before, value, after], axis=dim)
    return value


def gradients(padded):
    step_x = (padded[:, 2:, 1:-1, 1:-1] - padded[:, :-2, 1:-1, 1:-1]) * 0.5
    step_y = (padded[:, 1:-1, 2:, 1:-1] - padded[:, 1:-1, :-2, 1:-1]) * 0.5
    step_z = (padded[:, 1:-1, 1:-1, 2:] - padded[:, 1:-1, 1:-1, :-2]) * 0.5
    return jnp.stack([step_x, step_y, step_z], axis=1)


def face_gradients(value):
    steps = []
    for axis, dim in (("gx", 1), ("gy", 2), ("gz", 3)):
        peers, length = lax.axis_size(axis), value.shape[dim]
        up = [(i, (i + 1) % peers) for i in range(peers)]
        down = [(j, i) for i, j in up]
        before = lax.ppermute(lax.slice_in_dim(value, length - 1, length, axis=dim), axis, up)
        after = lax.ppermute(lax.slice_in_dim(value, 0, 1, axis=dim), axis, down)
        if axis == "gz":
            level = lax.axis_index(axis)
            before = jnp.where(level == 0, jnp.float32(0.0), before)
            after = jnp.where(level == peers - 1, jnp.float32(0.0), after)
        ext = jnp.concatenate([before, value, after], axis=dim)
        high = lax.slice_in_dim(ext, 2, length + 2, axis=dim)
        low = lax.slice_in_dim(ext, 0, length, axis=dim)
        steps.append((high - low) * 0.5)
    return jnp.stack(steps, axis=1)


def halving_stages(axes):
    stages = []
    for axis in axes:
        size = lax.axis_size(axis)
        bit = size // 2
        while bit >= 1:
            stages.append((axis, bit, size))
            bit //= 2
    return stages


def halve(value, axis, bit, size, dim):
    pairs = [(i, i ^ bit) for i in range(size)]
    mine = (lax.axis_index(axis) // bit) % 2
    keep = lax.dynamic_index_in_dim(value, mine, dim, keepdims=True)
    other = lax.dynamic_index_in_dim(value, 1 - mine, dim, keepdims=True)
    return keep + lax.ppermute(other, axis, pairs)


def scatter_sum(payload, axes):
    sizes = [lax.axis_size(a) for a in axes]
    if any(s & (s - 1) for s in sizes):
        return lax.psum_scatter(payload, tuple(axes), scatter_dimension=0, tiled=True)
    stages = halving_stages(axes)
    rows, lanes = payload.shape[1], payload.shape[2]
    value = payload.reshape((2,) * len(stages) + (rows, lanes))
    first = [k for k, s in enumerate(stages) if s[0] == axes[-1]]
    for k in first:
        value = halve(value, *stages[k], k)
    rest = [k for k in range(len(stages)) if k not in first]
    tail = rest[:1] if rest and stages[rest[0]][1] > 1 else []
    head = [k for k in rest if k not in tail][::-1]
    count = min(3, len(rest), rows)
    cuts = np.array_split(np.arange(rows), count) if count else [np.arange(rows)]
    parts = []
    for p, cut in enumerate(cuts):
        part = value[..., int(cut[0]) : int(cut[-1]) + 1, :]
        turn = p % len(head) if head else 0
        for k in head[turn:] + head[:turn] + tail:
            part = halve(part, *stages[k], k)
        parts.append(part)
    value = jnp.concatenate(parts, axis=-2) if len(parts) > 1 else parts[0]
    return value.reshape(1, rows, lanes)


def triangle_kernel(block_len, slot_ref, w_ref, g_ref, m_ref, out_ref, sym_ref):
    test, width = w_ref.shape[1], m_ref.shape[1]
    group = 4
    out_ref[...] = jnp.zeros(out_ref.shape, out_ref.dtype)

    def contract(step, carry):
        slabs = []
        for u in range(group):
            i = step * group + u
            zt = w_ref[0, pl.ds(i, 1), :] * g_ref[0]
            zt = zt + w_ref[1, pl.ds(i, 1), :] * g_ref[1]
            zt = zt + w_ref[2, pl.ds(i, 1), :] * g_ref[2]
            slabs.append(zt)
        zt = jnp.concatenate(slabs, axis=0)
        part = jnp.dot(zt, m_ref[...], precision=lax.Precision.HIGHEST, preferred_element_type=jnp.float32)
        for u in range(group):
            piece = part[u * width : (u + 1) * width, :]
            start = pl.multiple_of((step * group + u) * width, width)
            sym_ref[pl.ds(start, width), :] = piece + piece.T
        return carry

    lax.fori_loop(0, test // group, contract, 0)
    lane = lax.broadcasted_iota(jnp.int32, (test, 128), 1)
    for j in range(width):
        slab = sym_ref[pl.ds(j, test, stride=width), :]
        offset = j * width - (j * (j - 1)) // 2
        stop = offset + width - j
        for c in range(offset // block_len, (stop - 1) // block_len + 1):
            lo = max(offset, c * block_len) - c * block_len
            hi = min(stop, (c + 1) * block_len) - c * block_len
            slot = slot_ref[c]
            for u in range(lo // 128, (hi - 1) // 128 + 1):
                base = c * block_len + u * 128
                rolled = pltpu.roll(slab, (offset - j - base) % 128, 1)
                keep = (lane >= lo - u * 128) & (lane < hi - u * 128)
                cur = out_ref[slot, :, pl.ds(u * 128, 128)]
                out_ref[slot, :, pl.ds(u * 128, 128)] = jnp.where(keep, rolled, cur)


def triangle(slots, weighted, grads, modes_flat, block_len):
    owners = slots.shape[0]
    test, width = weighted.shape[1], modes_flat.shape[1]
    tiles = -(-block_len // 128)
    return pl.pallas_call(
        functools.partial(triangle_kernel, block_len),
        out_shape=jax.ShapeDtypeStruct((owners, test, tiles * 128), jnp.float32),
        in_specs=[pl.BlockSpec(memory_space=pltpu.SMEM)] + [pl.BlockSpec(memory_space=pltpu.VMEM)] * 3,
        out_specs=pl.BlockSpec(memory_space=pltpu.VMEM),
        scratch_shapes=[pltpu.VMEM((test * width, width), jnp.float32)],
    )(slots, weighted, grads, modes_flat)


def shards(modes, cell_weight, pair_owner):
    width = modes.shape[4]
    size_x = lax.axis_size("gx")
    size_y = lax.axis_size("gy")
    size_z = lax.axis_size("gz")
    owners = size_x * size_y * size_z
    grads = face_gradients(modes)
    mode_flat = modes.reshape(3, -1, width)
    grad_flat = grads.reshape(3, 3, -1, width)
    weight_flat = cell_weight.reshape(-1)
    total_cells = modes.shape[1] * modes.shape[2] * modes.shape[3] * owners
    scale = 1.0 / jnp.sqrt(jnp.float32(3.0 * total_cells))
    cells = mode_flat.shape[1]
    weighted = mode_flat[:, :, :TEST] * (weight_flat * scale)[None, :, None]
    weighted = jnp.tile(jnp.swapaxes(weighted, 1, 2), (1, 1, 3))
    grads_t = grad_flat.transpose(0, 3, 1, 2).reshape(3, width, 3 * cells)
    pair_total = width * (width + 1) // 2
    block_len = (pair_total + owners - 1) // owners
    ranks = jnp.arange(owners, dtype=jnp.int32)
    slots = jnp.sum(jnp.where(pair_owner[None, :] == ranks[:, None], ranks[None, :], 0), axis=1)
    slots = jnp.clip(slots, 0, owners - 1).astype(jnp.int32)
    placed = triangle(slots, weighted, grads_t, mode_flat.reshape(3 * cells, width), block_len)
    partial_terms = placed[:, :, :block_len].reshape(owners, TEST * block_len)
    lanes = 128
    rows = -(-TEST * block_len // lanes)
    partial_terms = jnp.pad(partial_terms, ((0, 0), (0, rows * lanes - TEST * block_len)))
    owned = scatter_sum(partial_terms.reshape(owners, rows, lanes), ("gx", "gy", "gz"))
    return owned.reshape(-1)[: TEST * block_len].reshape(TEST, block_len)


def solution(mesh):
    placed = (P("groups", "gx", "gy", "gz", None), P("gx", "gy", "gz"), P())
    return jax.shard_map(
        shards,
        mesh=mesh,
        in_specs=placed,
        out_specs=P("groups", ("gx", "gy", "gz")),
        check_vma=False,
    )
```

```python
import functools

import jax
import jax.numpy as jnp
import numpy as np
from jax import lax
from jax.experimental import pallas as pl
from jax.experimental.pallas import tpu as pltpu
from jax.sharding import PartitionSpec as P

TEST = 64


def extended(value, sides, width):
    for axis, dim in sides:
        peers, length = (lax.axis_size(axis), value.shape[dim])
        up = [(i, (i + 1) % peers) for i in range(peers)]
        down = [(j, i) for i, j in up]
        last = lax.slice_in_dim(value, length - width, length, axis=dim)
        leading = lax.slice_in_dim(value, 0, width, axis=dim)
        before = lax.ppermute(last, axis, up)
        after = lax.ppermute(leading, axis, down)
        value = jnp.concatenate([before, value, after], axis=dim)
    return value


def gradients(padded):
    step_x = (padded[:, 2:, 1:-1, 1:-1] - padded[:, :-2, 1:-1, 1:-1]) * 0.5
    step_y = (padded[:, 1:-1, 2:, 1:-1] - padded[:, 1:-1, :-2, 1:-1]) * 0.5
    step_z = (padded[:, 1:-1, 1:-1, 2:] - padded[:, 1:-1, 1:-1, :-2]) * 0.5
    return jnp.stack([step_x, step_y, step_z], axis=1)


def face_gradients(value):
    steps = []
    for axis, dim in (("gx", 1), ("gy", 2), ("gz", 3)):
        peers, length = lax.axis_size(axis), value.shape[dim]
        up = [(i, (i + 1) % peers) for i in range(peers)]
        down = [(j, i) for i, j in up]
        before = lax.ppermute(lax.slice_in_dim(value, length - 1, length, axis=dim), axis, up)
        after = lax.ppermute(lax.slice_in_dim(value, 0, 1, axis=dim), axis, down)
        if axis == "gz":
            level = lax.axis_index(axis)
            before = jnp.where(level == 0, jnp.float32(0.0), before)
            after = jnp.where(level == peers - 1, jnp.float32(0.0), after)
        ext = jnp.concatenate([before, value, after], axis=dim)
        high = lax.slice_in_dim(ext, 2, length + 2, axis=dim)
        low = lax.slice_in_dim(ext, 0, length, axis=dim)
        steps.append((high - low) * 0.5)
    return jnp.stack(steps, axis=1)


def halving_stages(axes):
    stages = []
    for axis in axes:
        size = lax.axis_size(axis)
        bit = size // 2
        while bit >= 1:
            stages.append((axis, bit, size))
            bit //= 2
    return stages


def halve(value, axis, bit, size, dim):
    pairs = [(i, i ^ bit) for i in range(size)]
    mine = (lax.axis_index(axis) // bit) % 2
    keep = lax.dynamic_index_in_dim(value, mine, dim, keepdims=True)
    other = lax.dynamic_index_in_dim(value, 1 - mine, dim, keepdims=True)
    return keep + lax.ppermute(other, axis, pairs)


def scatter_sum(payload, axes):
    sizes = [lax.axis_size(a) for a in axes]
    if any(s & (s - 1) for s in sizes):
        return lax.psum_scatter(payload, tuple(axes), scatter_dimension=0, tiled=True)
    stages = halving_stages(axes)
    rows, lanes = payload.shape[1], payload.shape[2]
    value = payload.reshape((2,) * len(stages) + (rows, lanes))
    first = [k for k, s in enumerate(stages) if s[0] == axes[-1]]
    for k in first:
        value = halve(value, *stages[k], k)
    rest = [k for k in range(len(stages)) if k not in first]
    tail = rest[:1] if rest and stages[rest[0]][1] > 1 else []
    head = [k for k in rest if k not in tail][::-1]
    count = min(3, len(rest), rows)
    cuts = np.array_split(np.arange(rows), count) if count else [np.arange(rows)]
    parts = []
    for p, cut in enumerate(cuts):
        part = value[..., int(cut[0]) : int(cut[-1]) + 1, :]
        turn = p % len(head) if head else 0
        for k in head[turn:] + head[:turn] + tail:
            part = halve(part, *stages[k], k)
        parts.append(part)
    value = jnp.concatenate(parts, axis=-2) if len(parts) > 1 else parts[0]
    return value.reshape(1, rows, lanes)


def triangle_kernel(block_len, slot_ref, w_ref, g_ref, m_ref, out_ref, sym_ref):
    test, width = w_ref.shape[1], m_ref.shape[1]
    group = 4
    out_ref[...] = jnp.zeros(out_ref.shape, out_ref.dtype)

    def contract(step, carry):
        slabs = []
        for u in range(group):
            i = step * group + u
            zt = w_ref[0, pl.ds(i, 1), :] * g_ref[0]
            zt = zt + w_ref[1, pl.ds(i, 1), :] * g_ref[1]
            zt = zt + w_ref[2, pl.ds(i, 1), :] * g_ref[2]
            slabs.append(zt)
        zt = jnp.concatenate(slabs, axis=0)
        part = jnp.dot(zt, m_ref[...], precision=lax.Precision.HIGH, preferred_element_type=jnp.float32)
        for u in range(group):
            piece = part[u * width : (u + 1) * width, :]
            start = pl.multiple_of((step * group + u) * width, width)
            sym_ref[pl.ds(start, width), :] = piece + piece.T
        return carry

    lax.fori_loop(0, test // group, contract, 0)
    lane = lax.broadcasted_iota(jnp.int32, (test, 128), 1)
    for j in range(width):
        slab = sym_ref[pl.ds(j, test, stride=width), :]
        offset = j * width - (j * (j - 1)) // 2
        stop = offset + width - j
        for c in range(offset // block_len, (stop - 1) // block_len + 1):
            lo = max(offset, c * block_len) - c * block_len
            hi = min(stop, (c + 1) * block_len) - c * block_len
            slot = slot_ref[c]
            for u in range(lo // 128, (hi - 1) // 128 + 1):
                base = c * block_len + u * 128
                rolled = pltpu.roll(slab, (offset - j - base) % 128, 1)
                keep = (lane >= lo - u * 128) & (lane < hi - u * 128)
                cur = out_ref[slot, :, pl.ds(u * 128, 128)]
                out_ref[slot, :, pl.ds(u * 128, 128)] = jnp.where(keep, rolled, cur)


def triangle(slots, weighted, grads, modes_flat, block_len):
    owners = slots.shape[0]
    test, width = weighted.shape[1], modes_flat.shape[1]
    tiles = -(-block_len // 128)
    return pl.pallas_call(
        functools.partial(triangle_kernel, block_len),
        out_shape=jax.ShapeDtypeStruct((owners, test, tiles * 128), jnp.float32),
        in_specs=[pl.BlockSpec(memory_space=pltpu.SMEM)] + [pl.BlockSpec(memory_space=pltpu.VMEM)] * 3,
        out_specs=pl.BlockSpec(memory_space=pltpu.VMEM),
        scratch_shapes=[pltpu.VMEM((test * width, width), jnp.float32)],
    )(slots, weighted, grads, modes_flat)


def shards(modes, cell_weight, pair_owner):
    width = modes.shape[4]
    size_x = lax.axis_size("gx")
    size_y = lax.axis_size("gy")
    size_z = lax.axis_size("gz")
    owners = size_x * size_y * size_z
    grads = face_gradients(modes)
    mode_flat = modes.reshape(3, -1, width)
    grad_flat = grads.reshape(3, 3, -1, width)
    weight_flat = cell_weight.reshape(-1)
    total_cells = modes.shape[1] * modes.shape[2] * modes.shape[3] * owners
    scale = 1.0 / jnp.sqrt(jnp.float32(3.0 * total_cells))
    cells = mode_flat.shape[1]
    weighted = mode_flat[:, :, :TEST] * (weight_flat * scale)[None, :, None]
    weighted = jnp.tile(jnp.swapaxes(weighted, 1, 2), (1, 1, 3))
    grads_t = grad_flat.transpose(0, 3, 1, 2).reshape(3, width, 3 * cells)
    pair_total = width * (width + 1) // 2
    block_len = (pair_total + owners - 1) // owners
    ranks = jnp.arange(owners, dtype=jnp.int32)
    slots = jnp.sum(jnp.where(pair_owner[None, :] == ranks[:, None], ranks[None, :], 0), axis=1)
    slots = jnp.clip(slots, 0, owners - 1).astype(jnp.int32)
    placed = triangle(slots, weighted, grads_t, mode_flat.reshape(3 * cells, width), block_len)
    partial_terms = placed[:, :, :block_len].reshape(owners, TEST * block_len)
    lanes = 128
    rows = -(-TEST * block_len // lanes)
    partial_terms = jnp.pad(partial_terms, ((0, 0), (0, rows * lanes - TEST * block_len)))
    owned = scatter_sum(partial_terms.reshape(owners, rows, lanes), ("gx", "gy", "gz"))
    return owned.reshape(-1)[: TEST * block_len].reshape(TEST, block_len)


def solution(mesh):
    placed = (P("groups", "gx", "gy", "gz", None), P("gx", "gy", "gz"), P())
    return jax.shard_map(
        shards,
        mesh=mesh,
        in_specs=placed,
        out_specs=P("groups", ("gx", "gy", "gz")),
        check_vma=False,
    )
```

```python
import functools

import jax
import jax.numpy as jnp
import numpy as np
from jax import lax
from jax.experimental import pallas as pl
from jax.experimental.pallas import tpu as pltpu
from jax.sharding import PartitionSpec as P

TEST = 64


def extended(value, sides, width):
    for axis, dim in sides:
        peers, length = (lax.axis_size(axis), value.shape[dim])
        up = [(i, (i + 1) % peers) for i in range(peers)]
        down = [(j, i) for i, j in up]
        last = lax.slice_in_dim(value, length - width, length, axis=dim)
        leading = lax.slice_in_dim(value, 0, width, axis=dim)
        before = lax.ppermute(last, axis, up)
        after = lax.ppermute(leading, axis, down)
        value = jnp.concatenate([before, value, after], axis=dim)
    return value


def gradients(padded):
    step_x = (padded[:, 2:, 1:-1, 1:-1] - padded[:, :-2, 1:-1, 1:-1]) * 0.5
    step_y = (padded[:, 1:-1, 2:, 1:-1] - padded[:, 1:-1, :-2, 1:-1]) * 0.5
    step_z = (padded[:, 1:-1, 1:-1, 2:] - padded[:, 1:-1, 1:-1, :-2]) * 0.5
    return jnp.stack([step_x, step_y, step_z], axis=1)


def face_gradients(value):
    steps = []
    for axis, dim in (("gx", 1), ("gy", 2), ("gz", 3)):
        peers, length = lax.axis_size(axis), value.shape[dim]
        up = [(i, (i + 1) % peers) for i in range(peers)]
        down = [(j, i) for i, j in up]
        last = lax.slice_in_dim(value, length - 1, length, axis=dim)
        leading = lax.slice_in_dim(value, 0, 1, axis=dim)
        if axis == "gz" and peers == 2:
            level = lax.axis_index(axis)
            got = lax.ppermute(jnp.where(level == 0, last, leading), axis, [(0, 1), (1, 0)])
            before = jnp.where(level == 1, got, jnp.float32(0.0))
            after = jnp.where(level == 0, got, jnp.float32(0.0))
        else:
            before = lax.ppermute(last, axis, up)
            after = lax.ppermute(leading, axis, down)
            if axis == "gz":
                level = lax.axis_index(axis)
                before = jnp.where(level == 0, jnp.float32(0.0), before)
                after = jnp.where(level == peers - 1, jnp.float32(0.0), after)
        ext = jnp.concatenate([before, value, after], axis=dim)
        high = lax.slice_in_dim(ext, 2, length + 2, axis=dim)
        low = lax.slice_in_dim(ext, 0, length, axis=dim)
        steps.append((high - low) * 0.5)
    return jnp.stack(steps, axis=1)


def halving_stages(axes):
    stages = []
    for axis in axes:
        size = lax.axis_size(axis)
        bit = size // 2
        while bit >= 1:
            stages.append((axis, bit, size))
            bit //= 2
    return stages


def halve(value, axis, bit, size, dim):
    pairs = [(i, i ^ bit) for i in range(size)]
    mine = (lax.axis_index(axis) // bit) % 2
    keep = lax.dynamic_index_in_dim(value, mine, dim, keepdims=True)
    other = lax.dynamic_index_in_dim(value, 1 - mine, dim, keepdims=True)
    return keep + lax.ppermute(other, axis, pairs)


def scatter_sum(payload, axes):
    sizes = [lax.axis_size(a) for a in axes]
    if any(s & (s - 1) for s in sizes):
        return lax.psum_scatter(payload, tuple(axes), scatter_dimension=0, tiled=True)
    stages = halving_stages(axes)
    rows, lanes = payload.shape[1], payload.shape[2]
    value = payload.reshape((2,) * len(stages) + (rows, lanes))
    first = [k for k, s in enumerate(stages) if s[0] == axes[-1]]
    for k in first:
        value = halve(value, *stages[k], k)
    rest = [k for k in range(len(stages)) if k not in first]
    tail = rest[:1] if rest and stages[rest[0]][1] > 1 else []
    head = [k for k in rest if k not in tail][::-1]
    count = min(3, len(rest), rows)
    cuts = np.array_split(np.arange(rows), count) if count else [np.arange(rows)]
    parts = []
    for p, cut in enumerate(cuts):
        part = value[..., int(cut[0]) : int(cut[-1]) + 1, :]
        turn = p % len(head) if head else 0
        for k in head[turn:] + head[:turn] + tail:
            part = halve(part, *stages[k], k)
        parts.append(part)
    value = jnp.concatenate(parts, axis=-2) if len(parts) > 1 else parts[0]
    return value.reshape(1, rows, lanes)


def triangle_kernel(block_len, slot_ref, w_ref, g_ref, m_ref, out_ref, sym_ref):
    test, width = w_ref.shape[1], m_ref.shape[1]
    group = 4
    out_ref[...] = jnp.zeros(out_ref.shape, out_ref.dtype)

    def contract(step, carry):
        slabs = []
        for u in range(group):
            i = step * group + u
            zt = w_ref[0, pl.ds(i, 1), :] * g_ref[0]
            zt = zt + w_ref[1, pl.ds(i, 1), :] * g_ref[1]
            zt = zt + w_ref[2, pl.ds(i, 1), :] * g_ref[2]
            slabs.append(zt)
        zt = jnp.concatenate(slabs, axis=0)
        part = jnp.dot(zt, m_ref[...], precision=lax.Precision.HIGH, preferred_element_type=jnp.float32)
        for u in range(group):
            piece = part[u * width : (u + 1) * width, :]
            start = pl.multiple_of((step * group + u) * width, width)
            sym_ref[pl.ds(start, width), :] = piece + piece.T
        return carry

    lax.fori_loop(0, test // group, contract, 0)
    lane = lax.broadcasted_iota(jnp.int32, (test, 128), 1)
    for j in range(width):
        slab = sym_ref[pl.ds(j, test, stride=width), :]
        offset = j * width - (j * (j - 1)) // 2
        stop = offset + width - j
        for c in range(offset // block_len, (stop - 1) // block_len + 1):
            lo = max(offset, c * block_len) - c * block_len
            hi = min(stop, (c + 1) * block_len) - c * block_len
            slot = slot_ref[c]
            for u in range(lo // 128, (hi - 1) // 128 + 1):
                base = c * block_len + u * 128
                rolled = pltpu.roll(slab, (offset - j - base) % 128, 1)
                keep = (lane >= lo - u * 128) & (lane < hi - u * 128)
                cur = out_ref[slot, :, pl.ds(u * 128, 128)]
                out_ref[slot, :, pl.ds(u * 128, 128)] = jnp.where(keep, rolled, cur)


def triangle(slots, weighted, grads, modes_flat, block_len):
    owners = slots.shape[0]
    test, width = weighted.shape[1], modes_flat.shape[1]
    tiles = -(-block_len // 128)
    return pl.pallas_call(
        functools.partial(triangle_kernel, block_len),
        out_shape=jax.ShapeDtypeStruct((owners, test, tiles * 128), jnp.float32),
        in_specs=[pl.BlockSpec(memory_space=pltpu.SMEM)] + [pl.BlockSpec(memory_space=pltpu.VMEM)] * 3,
        out_specs=pl.BlockSpec(memory_space=pltpu.VMEM),
        scratch_shapes=[pltpu.VMEM((test * width, width), jnp.float32)],
    )(slots, weighted, grads, modes_flat)


def shards(modes, cell_weight, pair_owner):
    width = modes.shape[4]
    size_x = lax.axis_size("gx")
    size_y = lax.axis_size("gy")
    size_z = lax.axis_size("gz")
    owners = size_x * size_y * size_z
    grads = face_gradients(modes)
    mode_flat = modes.reshape(3, -1, width)
    grad_flat = grads.reshape(3, 3, -1, width)
    weight_flat = cell_weight.reshape(-1)
    total_cells = modes.shape[1] * modes.shape[2] * modes.shape[3] * owners
    scale = 1.0 / jnp.sqrt(jnp.float32(3.0 * total_cells))
    cells = mode_flat.shape[1]
    weighted = mode_flat[:, :, :TEST] * (weight_flat * scale)[None, :, None]
    weighted = jnp.tile(jnp.swapaxes(weighted, 1, 2), (1, 1, 3))
    grads_t = grad_flat.transpose(0, 3, 1, 2).reshape(3, width, 3 * cells)
    pair_total = width * (width + 1) // 2
    block_len = (pair_total + owners - 1) // owners
    ranks = jnp.arange(owners, dtype=jnp.int32)
    slots = jnp.sum(jnp.where(pair_owner[None, :] == ranks[:, None], ranks[None, :], 0), axis=1)
    slots = jnp.clip(slots, 0, owners - 1).astype(jnp.int32)
    placed = triangle(slots, weighted, grads_t, mode_flat.reshape(3 * cells, width), block_len)
    partial_terms = placed[:, :, :block_len].reshape(owners, TEST * block_len)
    lanes = 128
    rows = -(-TEST * block_len // lanes)
    partial_terms = jnp.pad(partial_terms, ((0, 0), (0, rows * lanes - TEST * block_len)))
    owned = scatter_sum(partial_terms.reshape(owners, rows, lanes), ("gx", "gy", "gz"))
    return owned.reshape(-1)[: TEST * block_len].reshape(TEST, block_len)


def solution(mesh):
    placed = (P("groups", "gx", "gy", "gz", None), P("gx", "gy", "gz"), P())
    return jax.shard_map(
        shards,
        mesh=mesh,
        in_specs=placed,
        out_specs=P("groups", ("gx", "gy", "gz")),
        check_vma=False,
    )
```

```python
import functools

import jax
import jax.numpy as jnp
import numpy as np
from jax import lax
from jax.experimental import pallas as pl
from jax.experimental.pallas import tpu as pltpu
from jax.sharding import PartitionSpec as P

TEST = 64


def extended(value, sides, width):
    for axis, dim in sides:
        peers, length = (lax.axis_size(axis), value.shape[dim])
        up = [(i, (i + 1) % peers) for i in range(peers)]
        down = [(j, i) for i, j in up]
        last = lax.slice_in_dim(value, length - width, length, axis=dim)
        leading = lax.slice_in_dim(value, 0, width, axis=dim)
        before = lax.ppermute(last, axis, up)
        after = lax.ppermute(leading, axis, down)
        value = jnp.concatenate([before, value, after], axis=dim)
    return value


def gradients(padded):
    step_x = (padded[:, 2:, 1:-1, 1:-1] - padded[:, :-2, 1:-1, 1:-1]) * 0.5
    step_y = (padded[:, 1:-1, 2:, 1:-1] - padded[:, 1:-1, :-2, 1:-1]) * 0.5
    step_z = (padded[:, 1:-1, 1:-1, 2:] - padded[:, 1:-1, 1:-1, :-2]) * 0.5
    return jnp.stack([step_x, step_y, step_z], axis=1)


def face_gradients(value):
    steps = []
    for axis, dim in (("gx", 1), ("gy", 2), ("gz", 3)):
        peers, length = lax.axis_size(axis), value.shape[dim]
        up = [(i, (i + 1) % peers) for i in range(peers)]
        down = [(j, i) for i, j in up]
        last = lax.slice_in_dim(value, length - 1, length, axis=dim)
        leading = lax.slice_in_dim(value, 0, 1, axis=dim)
        if axis == "gz" and peers == 2:
            level = lax.axis_index(axis)
            got = lax.ppermute(jnp.where(level == 0, last, leading), axis, [(0, 1), (1, 0)])
            before = jnp.where(level == 1, got, jnp.float32(0.0))
            after = jnp.where(level == 0, got, jnp.float32(0.0))
        else:
            before = lax.ppermute(last, axis, up)
            after = lax.ppermute(leading, axis, down)
            if axis == "gz":
                level = lax.axis_index(axis)
                before = jnp.where(level == 0, jnp.float32(0.0), before)
                after = jnp.where(level == peers - 1, jnp.float32(0.0), after)
        ext = jnp.concatenate([before, value, after], axis=dim)
        high = lax.slice_in_dim(ext, 2, length + 2, axis=dim)
        low = lax.slice_in_dim(ext, 0, length, axis=dim)
        steps.append((high - low) * 0.5)
    return jnp.stack(steps, axis=1)


def halving_stages(axes):
    stages = []
    for axis in axes:
        size = lax.axis_size(axis)
        bit = size // 2
        while bit >= 1:
            stages.append((axis, bit, size))
            bit //= 2
    return stages


def halve(value, axis, bit, size, dim):
    pairs = [(i, i ^ bit) for i in range(size)]
    mine = (lax.axis_index(axis) // bit) % 2
    keep = lax.dynamic_index_in_dim(value, mine, dim, keepdims=True)
    other = lax.dynamic_index_in_dim(value, 1 - mine, dim, keepdims=True)
    return keep + lax.ppermute(other, axis, pairs)


def scatter_sum(payload, axes):
    sizes = [lax.axis_size(a) for a in axes]
    if any(s & (s - 1) for s in sizes):
        return lax.psum_scatter(payload, tuple(axes), scatter_dimension=0, tiled=True)
    stages = halving_stages(axes)
    rows, lanes = payload.shape[1], payload.shape[2]
    value = payload.reshape((2,) * len(stages) + (rows, lanes))
    first = [k for k, s in enumerate(stages) if s[0] == axes[-1]]
    for k in first:
        value = halve(value, *stages[k], k)
    rest = [k for k in range(len(stages)) if k not in first]
    tail = rest[:1] if rest and stages[rest[0]][1] > 1 else []
    head = [k for k in rest if k not in tail][::-1]
    count = min(3, len(rest), rows)
    cuts = np.array_split(np.arange(rows), count) if count else [np.arange(rows)]
    parts = []
    for p, cut in enumerate(cuts):
        part = value[..., int(cut[0]) : int(cut[-1]) + 1, :]
        turn = p % len(head) if head else 0
        for k in head[turn:] + head[:turn] + tail:
            part = halve(part, *stages[k], k)
        parts.append(part)
    value = jnp.concatenate(parts, axis=-2) if len(parts) > 1 else parts[0]
    return value.reshape(1, rows, lanes)


def triangle_kernel(block_len, dense, slot_ref, w_ref, g_ref, m_ref, out_ref, sym_ref, rest_ref):
    test, width = w_ref.shape[1], m_ref.shape[1]
    group = 4
    full = block_len // 128 if dense else out_ref.shape[2] // 128
    out_ref[...] = jnp.zeros(out_ref.shape, out_ref.dtype)
    rest_ref[...] = jnp.zeros(rest_ref.shape, rest_ref.dtype)

    def contract(step, carry):
        slabs = []
        for u in range(group):
            i = step * group + u
            zt = w_ref[0, pl.ds(i, 1), :] * g_ref[0]
            zt = zt + w_ref[1, pl.ds(i, 1), :] * g_ref[1]
            zt = zt + w_ref[2, pl.ds(i, 1), :] * g_ref[2]
            slabs.append(zt)
        zt = jnp.concatenate(slabs, axis=0)
        part = jnp.dot(zt, m_ref[...], precision=lax.Precision.HIGH, preferred_element_type=jnp.float32)
        for u in range(group):
            piece = part[u * width : (u + 1) * width, :]
            start = pl.multiple_of((step * group + u) * width, width)
            sym_ref[pl.ds(start, width), :] = piece + piece.T
        return carry

    lax.fori_loop(0, test // group, contract, 0)
    lane = lax.broadcasted_iota(jnp.int32, (test, 128), 1)
    for j in range(width):
        slab = sym_ref[pl.ds(j, test, stride=width), :]
        offset = j * width - (j * (j - 1)) // 2
        stop = offset + width - j
        for c in range(offset // block_len, (stop - 1) // block_len + 1):
            lo = max(offset, c * block_len) - c * block_len
            hi = min(stop, (c + 1) * block_len) - c * block_len
            slot = slot_ref[c]
            for u in range(lo // 128, (hi - 1) // 128 + 1):
                base = c * block_len + u * 128
                rolled = pltpu.roll(slab, (offset - j - base) % 128, 1)
                keep = (lane >= lo - u * 128) & (lane < hi - u * 128)
                if u < full and dense:
                    target = out_ref.at[slot, pl.ds(u * test, test), :]
                elif u < full:
                    target = out_ref.at[slot, :, pl.ds(u * 128, 128)]
                else:
                    target = rest_ref.at[slot]
                target[...] = jnp.where(keep, rolled, target[...])
    if dense:
        spare = block_len - full * 128
        row = lax.broadcasted_iota(jnp.int32, (test, 128), 0)
        for s in range(out_ref.shape[0]):
            tail = rest_ref[s]
            picked = jnp.zeros((test, 128), jnp.float32)
            for r in range(spare):
                hit = (lane >= r * test) & (lane < (r + 1) * test) & (lane - r * test == row)
                picked = jnp.where(hit, jnp.broadcast_to(tail[:, r : r + 1], (test, 128)), picked)
            out_ref[s, pl.ds(full * test, 1), :] = jnp.sum(picked, axis=0, keepdims=True)


def triangle(slots, weighted, grads, modes_flat, block_len, dense):
    owners = slots.shape[0]
    test, width = weighted.shape[1], modes_flat.shape[1]
    tiles = -(-block_len // 128)
    if dense:
        shape = (owners, (block_len // 128) * test + 1, 128)
    else:
        shape = (owners, test, tiles * 128)
    return pl.pallas_call(
        functools.partial(triangle_kernel, block_len, dense),
        out_shape=jax.ShapeDtypeStruct(shape, jnp.float32),
        in_specs=[pl.BlockSpec(memory_space=pltpu.SMEM)] + [pl.BlockSpec(memory_space=pltpu.VMEM)] * 3,
        out_specs=pl.BlockSpec(memory_space=pltpu.VMEM),
        scratch_shapes=[
            pltpu.VMEM((test * width, width), jnp.float32),
            pltpu.VMEM((owners if dense else 1, test, 128), jnp.float32),
        ],
    )(slots, weighted, grads, modes_flat)


def shards(modes, cell_weight, pair_owner):
    width = modes.shape[4]
    size_x = lax.axis_size("gx")
    size_y = lax.axis_size("gy")
    size_z = lax.axis_size("gz")
    owners = size_x * size_y * size_z
    grads = face_gradients(modes)
    mode_flat = modes.reshape(3, -1, width)
    grad_flat = grads.reshape(3, 3, -1, width)
    weight_flat = cell_weight.reshape(-1)
    total_cells = modes.shape[1] * modes.shape[2] * modes.shape[3] * owners
    scale = 1.0 / jnp.sqrt(jnp.float32(3.0 * total_cells))
    cells = mode_flat.shape[1]
    weighted = mode_flat[:, :, :TEST] * (weight_flat * scale)[None, :, None]
    weighted = jnp.tile(jnp.swapaxes(weighted, 1, 2), (1, 1, 3))
    grads_t = grad_flat.transpose(0, 3, 1, 2).reshape(3, width, 3 * cells)
    pair_total = width * (width + 1) // 2
    block_len = (pair_total + owners - 1) // owners
    ranks = jnp.arange(owners, dtype=jnp.int32)
    slots = jnp.sum(jnp.where(pair_owner[None, :] == ranks[:, None], ranks[None, :], 0), axis=1)
    slots = jnp.clip(slots, 0, owners - 1).astype(jnp.int32)
    full, spare = block_len // 128, block_len % 128
    dense = 0 < spare and spare * TEST <= 128
    placed = triangle(slots, weighted, grads_t, mode_flat.reshape(3 * cells, width), block_len, dense)
    if dense:
        owned = scatter_sum(placed, ("gx", "gy", "gz"))[0]
        main = owned[: full * TEST].reshape(full, TEST, 128).transpose(1, 0, 2).reshape(TEST, full * 128)
        tail = owned[full * TEST, : spare * TEST].reshape(spare, TEST).T
        return jnp.concatenate([main, tail], axis=1)
    partial_terms = placed[:, :, :block_len].reshape(owners, TEST * block_len)
    lanes = 128
    rows = -(-TEST * block_len // lanes)
    partial_terms = jnp.pad(partial_terms, ((0, 0), (0, rows * lanes - TEST * block_len)))
    owned = scatter_sum(partial_terms.reshape(owners, rows, lanes), ("gx", "gy", "gz"))
    return owned.reshape(-1)[: TEST * block_len].reshape(TEST, block_len)

def solution(mesh):
    placed = (P("groups", "gx", "gy", "gz", None), P("gx", "gy", "gz"), P())
    return jax.shard_map(
        shards,
        mesh=mesh,
        in_specs=placed,
        out_specs=P("groups", ("gx", "gy", "gz")),
        check_vma=False,
    )
```

```python
import functools

import jax
import jax.numpy as jnp
import numpy as np
from jax import lax
from jax.experimental import pallas as pl
from jax.experimental.pallas import tpu as pltpu
from jax.sharding import PartitionSpec as P

TEST = 64


def extended(value, sides, width):
    for axis, dim in sides:
        peers, length = (lax.axis_size(axis), value.shape[dim])
        up = [(i, (i + 1) % peers) for i in range(peers)]
        down = [(j, i) for i, j in up]
        last = lax.slice_in_dim(value, length - width, length, axis=dim)
        leading = lax.slice_in_dim(value, 0, width, axis=dim)
        before = lax.ppermute(last, axis, up)
        after = lax.ppermute(leading, axis, down)
        value = jnp.concatenate([before, value, after], axis=dim)
    return value


def gradients(padded):
    step_x = (padded[:, 2:, 1:-1, 1:-1] - padded[:, :-2, 1:-1, 1:-1]) * 0.5
    step_y = (padded[:, 1:-1, 2:, 1:-1] - padded[:, 1:-1, :-2, 1:-1]) * 0.5
    step_z = (padded[:, 1:-1, 1:-1, 2:] - padded[:, 1:-1, 1:-1, :-2]) * 0.5
    return jnp.stack([step_x, step_y, step_z], axis=1)


def face_gradients(value):
    steps = []
    for axis, dim in (("gx", 1), ("gy", 2), ("gz", 3)):
        peers, length = lax.axis_size(axis), value.shape[dim]
        up = [(i, (i + 1) % peers) for i in range(peers)]
        down = [(j, i) for i, j in up]
        last = lax.slice_in_dim(value, length - 1, length, axis=dim)
        leading = lax.slice_in_dim(value, 0, 1, axis=dim)
        if axis == "gz" and peers == 2:
            level = lax.axis_index(axis)
            got = lax.ppermute(jnp.where(level == 0, last, leading), axis, [(0, 1), (1, 0)])
            before = jnp.where(level == 1, got, jnp.float32(0.0))
            after = jnp.where(level == 0, got, jnp.float32(0.0))
        else:
            before = lax.ppermute(last, axis, up)
            after = lax.ppermute(leading, axis, down)
            if axis == "gz":
                level = lax.axis_index(axis)
                before = jnp.where(level == 0, jnp.float32(0.0), before)
                after = jnp.where(level == peers - 1, jnp.float32(0.0), after)
        ext = jnp.concatenate([before, value, after], axis=dim)
        high = lax.slice_in_dim(ext, 2, length + 2, axis=dim)
        low = lax.slice_in_dim(ext, 0, length, axis=dim)
        steps.append((high - low) * 0.5)
    return jnp.stack(steps, axis=1)


def halving_stages(axes):
    stages = []
    for axis in axes:
        size = lax.axis_size(axis)
        bit = size // 2
        while bit >= 1:
            stages.append((axis, bit, size))
            bit //= 2
    return stages


def halve(value, axis, bit, size, dim):
    pairs = [(i, i ^ bit) for i in range(size)]
    mine = (lax.axis_index(axis) // bit) % 2
    keep = lax.dynamic_index_in_dim(value, mine, dim, keepdims=True)
    other = lax.dynamic_index_in_dim(value, 1 - mine, dim, keepdims=True)
    return keep + lax.ppermute(other, axis, pairs)


def scatter_sum(payload, axes, local=True):
    sizes = [lax.axis_size(a) for a in axes]
    if any(s & (s - 1) for s in sizes):
        return lax.psum_scatter(payload, tuple(axes), scatter_dimension=0, tiled=True)
    stages = halving_stages(axes)
    rows, lanes = payload.shape[1], payload.shape[2]
    value = payload.reshape((2,) * len(stages) + (rows, lanes))
    first = [k for k, s in enumerate(stages) if local and s[0] == axes[-1]]
    for k in first:
        value = halve(value, *stages[k], k)
    rest = [k for k in range(len(stages)) if k not in first]
    tail = rest[:1] if rest and stages[rest[0]][1] > 1 else []
    head = [k for k in rest if k not in tail][::-1]
    count = min(3, len(rest), rows)
    cuts = np.array_split(np.arange(rows), count) if count else [np.arange(rows)]
    parts = []
    for p, cut in enumerate(cuts):
        part = value[..., int(cut[0]) : int(cut[-1]) + 1, :]
        turn = p % len(head) if head else 0
        for k in head[turn:] + head[:turn] + tail:
            part = halve(part, *stages[k], k)
        parts.append(part)
    value = jnp.concatenate(parts, axis=-2) if len(parts) > 1 else parts[0]
    return value.reshape(1, rows, lanes)


def triangle_kernel(block_len, dense, slot_ref, side_ref, w_ref, g_ref, m_ref, out_ref, sym_ref, rest_ref):
    test, width = w_ref.shape[1], m_ref.shape[1]
    group = 4
    full = block_len // 128 if dense else out_ref.shape[2] // 128
    out_ref[...] = jnp.zeros(out_ref.shape, out_ref.dtype)
    rest_ref[...] = jnp.zeros(rest_ref.shape, rest_ref.dtype)

    def contract(step, carry):
        slabs = []
        for u in range(group):
            i = step * group + u
            zt = w_ref[0, pl.ds(i, 1), :] * g_ref[0]
            zt = zt + w_ref[1, pl.ds(i, 1), :] * g_ref[1]
            zt = zt + w_ref[2, pl.ds(i, 1), :] * g_ref[2]
            slabs.append(zt)
        zt = jnp.concatenate(slabs, axis=0)
        part = jnp.dot(zt, m_ref[...], precision=lax.Precision.HIGH, preferred_element_type=jnp.float32)
        for u in range(group):
            piece = part[u * width : (u + 1) * width, :]
            start = pl.multiple_of((step * group + u) * width, width)
            sym_ref[pl.ds(start, width), :] = piece + piece.T
        return carry

    lax.fori_loop(0, test // group, contract, 0)
    lane = lax.broadcasted_iota(jnp.int32, (test, 128), 1)
    for j in range(width):
        slab = sym_ref[pl.ds(j, test, stride=width), :]
        offset = j * width - (j * (j - 1)) // 2
        stop = offset + width - j
        for c in range(offset // block_len, (stop - 1) // block_len + 1):
            lo = max(offset, c * block_len) - c * block_len
            hi = min(stop, (c + 1) * block_len) - c * block_len
            slot = slot_ref[c]
            for u in range(lo // 128, (hi - 1) // 128 + 1):
                base = c * block_len + u * 128
                rolled = pltpu.roll(slab, (offset - j - base) % 128, 1)
                keep = (lane >= lo - u * 128) & (lane < hi - u * 128)
                if u < full and dense:
                    target = out_ref.at[(slot + side_ref[0]) % 2, slot // 2, pl.ds(u * test, test), :]
                elif u < full:
                    target = out_ref.at[slot, :, pl.ds(u * 128, 128)]
                else:
                    target = rest_ref.at[slot]
                target[...] = jnp.where(keep, rolled, target[...])
    if dense:
        spare = block_len - full * 128
        row = lax.broadcasted_iota(jnp.int32, (test, 128), 0)
        for s in range(rest_ref.shape[0]):
            tail = rest_ref[s]
            picked = jnp.zeros((test, 128), jnp.float32)
            for r in range(spare):
                hit = (lane >= r * test) & (lane < (r + 1) * test) & (lane - r * test == row)
                picked = jnp.where(hit, jnp.broadcast_to(tail[:, r : r + 1], (test, 128)), picked)
            out_ref[(s + side_ref[0]) % 2, s // 2, pl.ds(full * test, 1), :] = jnp.sum(picked, axis=0, keepdims=True)


def triangle(slots, side, weighted, grads, modes_flat, block_len, dense):
    owners = slots.shape[0]
    test, width = weighted.shape[1], modes_flat.shape[1]
    tiles = -(-block_len // 128)
    if dense:
        shape = (2, owners // 2, (block_len // 128) * test + 1, 128)
    else:
        shape = (owners, test, tiles * 128)
    return pl.pallas_call(
        functools.partial(triangle_kernel, block_len, dense),
        out_shape=jax.ShapeDtypeStruct(shape, jnp.float32),
        in_specs=[pl.BlockSpec(memory_space=pltpu.SMEM)] * 2 + [pl.BlockSpec(memory_space=pltpu.VMEM)] * 3,
        out_specs=pl.BlockSpec(memory_space=pltpu.VMEM),
        scratch_shapes=[
            pltpu.VMEM((test * width, width), jnp.float32),
            pltpu.VMEM((owners if dense else 1, test, 128), jnp.float32),
        ],
    )(slots, side, weighted, grads, modes_flat)


def shards(modes, cell_weight, pair_owner):
    width = modes.shape[4]
    size_x = lax.axis_size("gx")
    size_y = lax.axis_size("gy")
    size_z = lax.axis_size("gz")
    owners = size_x * size_y * size_z
    grads = face_gradients(modes)
    mode_flat = modes.reshape(3, -1, width)
    grad_flat = grads.reshape(3, 3, -1, width)
    weight_flat = cell_weight.reshape(-1)
    total_cells = modes.shape[1] * modes.shape[2] * modes.shape[3] * owners
    scale = 1.0 / jnp.sqrt(jnp.float32(3.0 * total_cells))
    cells = mode_flat.shape[1]
    weighted = mode_flat[:, :, :TEST] * (weight_flat * scale)[None, :, None]
    weighted = jnp.tile(jnp.swapaxes(weighted, 1, 2), (1, 1, 3))
    grads_t = grad_flat.transpose(0, 3, 1, 2).reshape(3, width, 3 * cells)
    pair_total = width * (width + 1) // 2
    block_len = (pair_total + owners - 1) // owners
    ranks = jnp.arange(owners, dtype=jnp.int32)
    slots = jnp.sum(jnp.where(pair_owner[None, :] == ranks[:, None], ranks[None, :], 0), axis=1)
    slots = jnp.clip(slots, 0, owners - 1).astype(jnp.int32)
    full, spare = block_len // 128, block_len % 128
    dense = 0 < spare and spare * TEST <= 128 and size_z == 2
    side = lax.axis_index("gz").astype(jnp.int32).reshape(1)
    placed = triangle(slots, side, weighted, grads_t, mode_flat.reshape(3 * cells, width), block_len, dense)
    if dense:
        merged = placed[0] + lax.ppermute(placed[1], "gz", [(0, 1), (1, 0)])
        owned = scatter_sum(merged, ("gx", "gy"), local=False)[0]
        main = owned[: full * TEST].reshape(full, TEST, 128).transpose(1, 0, 2).reshape(TEST, full * 128)
        tail = owned[full * TEST, : spare * TEST].reshape(spare, TEST).T
        return jnp.concatenate([main, tail], axis=1)
    partial_terms = placed[:, :, :block_len].reshape(owners, TEST * block_len)
    lanes = 128
    rows = -(-TEST * block_len // lanes)
    partial_terms = jnp.pad(partial_terms, ((0, 0), (0, rows * lanes - TEST * block_len)))
    owned = scatter_sum(partial_terms.reshape(owners, rows, lanes), ("gx", "gy", "gz"))
    return owned.reshape(-1)[: TEST * block_len].reshape(TEST, block_len)

def solution(mesh):
    placed = (P("groups", "gx", "gy", "gz", None), P("gx", "gy", "gz"), P())
    return jax.shard_map(
        shards,
        mesh=mesh,
        in_specs=placed,
        out_specs=P("groups", ("gx", "gy", "gz")),
        check_vma=False,
    )
```

```python
import functools

import jax
import jax.numpy as jnp
import numpy as np
from jax import lax
from jax.experimental import pallas as pl
from jax.experimental.pallas import tpu as pltpu
from jax.sharding import PartitionSpec as P

TEST = 64


def extended(value, sides, width):
    for axis, dim in sides:
        peers, length = (lax.axis_size(axis), value.shape[dim])
        up = [(i, (i + 1) % peers) for i in range(peers)]
        down = [(j, i) for i, j in up]
        last = lax.slice_in_dim(value, length - width, length, axis=dim)
        leading = lax.slice_in_dim(value, 0, width, axis=dim)
        before = lax.ppermute(last, axis, up)
        after = lax.ppermute(leading, axis, down)
        value = jnp.concatenate([before, value, after], axis=dim)
    return value


def gradients(padded):
    step_x = (padded[:, 2:, 1:-1, 1:-1] - padded[:, :-2, 1:-1, 1:-1]) * 0.5
    step_y = (padded[:, 1:-1, 2:, 1:-1] - padded[:, 1:-1, :-2, 1:-1]) * 0.5
    step_z = (padded[:, 1:-1, 1:-1, 2:] - padded[:, 1:-1, 1:-1, :-2]) * 0.5
    return jnp.stack([step_x, step_y, step_z], axis=1)


def face_gradients(value):
    steps = []
    for axis, dim in (("gx", 1), ("gy", 2), ("gz", 3)):
        peers, length = lax.axis_size(axis), value.shape[dim]
        up = [(i, (i + 1) % peers) for i in range(peers)]
        down = [(j, i) for i, j in up]
        last = lax.slice_in_dim(value, length - 1, length, axis=dim)
        leading = lax.slice_in_dim(value, 0, 1, axis=dim)
        if axis == "gz" and peers == 2:
            level = lax.axis_index(axis)
            got = lax.ppermute(jnp.where(level == 0, last, leading), axis, [(0, 1), (1, 0)])
            before = jnp.where(level == 1, got, jnp.float32(0.0))
            after = jnp.where(level == 0, got, jnp.float32(0.0))
        else:
            before = lax.ppermute(last, axis, up)
            after = lax.ppermute(leading, axis, down)
            if axis == "gz":
                level = lax.axis_index(axis)
                before = jnp.where(level == 0, jnp.float32(0.0), before)
                after = jnp.where(level == peers - 1, jnp.float32(0.0), after)
        ext = jnp.concatenate([before, value, after], axis=dim)
        high = lax.slice_in_dim(ext, 2, length + 2, axis=dim)
        low = lax.slice_in_dim(ext, 0, length, axis=dim)
        steps.append((high - low) * 0.5)
    return jnp.stack(steps, axis=1)


def halving_stages(axes):
    stages = []
    for axis in axes:
        size = lax.axis_size(axis)
        bit = size // 2
        while bit >= 1:
            stages.append((axis, bit, size))
            bit //= 2
    return stages


def halve(value, axis, bit, size, dim):
    pairs = [(i, i ^ bit) for i in range(size)]
    mine = (lax.axis_index(axis) // bit) % 2
    keep = lax.dynamic_index_in_dim(value, mine, dim, keepdims=True)
    other = lax.dynamic_index_in_dim(value, 1 - mine, dim, keepdims=True)
    return keep + lax.ppermute(other, axis, pairs)


def scatter_sum(payload, axes):
    sizes = [lax.axis_size(a) for a in axes]
    if any(s & (s - 1) for s in sizes):
        return lax.psum_scatter(payload, tuple(axes), scatter_dimension=0, tiled=True)
    stages = halving_stages(axes)
    rows, lanes = payload.shape[1], payload.shape[2]
    value = payload.reshape((2,) * len(stages) + (rows, lanes))
    first = [k for k, s in enumerate(stages) if s[0] == axes[-1]]
    for k in first:
        value = halve(value, *stages[k], k)
    rest = [k for k in range(len(stages)) if k not in first]
    tail = rest[:1] if rest and stages[rest[0]][1] > 1 else []
    head = [k for k in rest if k not in tail][::-1]
    count = min(3, len(rest), rows)
    cuts = np.array_split(np.arange(rows), count) if count else [np.arange(rows)]
    parts = []
    for p, cut in enumerate(cuts):
        part = value[..., int(cut[0]) : int(cut[-1]) + 1, :]
        turn = p % len(head) if head else 0
        for k in head[turn:] + head[:turn] + tail:
            part = halve(part, *stages[k], k)
        parts.append(part)
    value = jnp.concatenate(parts, axis=-2) if len(parts) > 1 else parts[0]
    return value.reshape(1, rows, lanes)


def triangle_kernel(block_len, dense, slot_ref, w_ref, g_ref, m_ref, out_ref, sym_ref, rest_ref):
    test, width = w_ref.shape[1], m_ref.shape[1]
    group = 8
    full = block_len // 128 if dense else out_ref.shape[2] // 128
    out_ref[...] = jnp.zeros(out_ref.shape, out_ref.dtype)
    rest_ref[...] = jnp.zeros(rest_ref.shape, rest_ref.dtype)

    def contract(step, carry):
        slabs = []
        for u in range(group):
            i = step * group + u
            zt = w_ref[0, pl.ds(i, 1), :] * g_ref[0]
            zt = zt + w_ref[1, pl.ds(i, 1), :] * g_ref[1]
            zt = zt + w_ref[2, pl.ds(i, 1), :] * g_ref[2]
            slabs.append(zt)
        zt = jnp.concatenate(slabs, axis=0)
        part = jnp.dot(zt, m_ref[...], precision=lax.Precision.HIGH, preferred_element_type=jnp.float32)
        for u in range(group):
            piece = part[u * width : (u + 1) * width, :]
            start = pl.multiple_of((step * group + u) * width, width)
            sym_ref[pl.ds(start, width), :] = piece + piece.T
        return carry

    lax.fori_loop(0, test // group, contract, 0)
    lane = lax.broadcasted_iota(jnp.int32, (test, 128), 1)
    for j in range(width):
        slab = sym_ref[pl.ds(j, test, stride=width), :]
        offset = j * width - (j * (j - 1)) // 2
        stop = offset + width - j
        for c in range(offset // block_len, (stop - 1) // block_len + 1):
            lo = max(offset, c * block_len) - c * block_len
            hi = min(stop, (c + 1) * block_len) - c * block_len
            slot = slot_ref[c]
            for u in range(lo // 128, (hi - 1) // 128 + 1):
                base = c * block_len + u * 128
                rolled = pltpu.roll(slab, (offset - j - base) % 128, 1)
                keep = (lane >= lo - u * 128) & (lane < hi - u * 128)
                if u < full and dense:
                    target = out_ref.at[slot, pl.ds(u * test, test), :]
                elif u < full:
                    target = out_ref.at[slot, :, pl.ds(u * 128, 128)]
                else:
                    target = rest_ref.at[slot]
                target[...] = jnp.where(keep, rolled, target[...])
    if dense:
        spare = block_len - full * 128
        row = lax.broadcasted_iota(jnp.int32, (test, 128), 0)
        for s in range(out_ref.shape[0]):
            tail = rest_ref[s]
            picked = jnp.zeros((test, 128), jnp.float32)
            for r in range(spare):
                hit = (lane >= r * test) & (lane < (r + 1) * test) & (lane - r * test == row)
                picked = jnp.where(hit, jnp.broadcast_to(tail[:, r : r + 1], (test, 128)), picked)
            out_ref[s, pl.ds(full * test, 1), :] = jnp.sum(picked, axis=0, keepdims=True)


def triangle(slots, weighted, grads, modes_flat, block_len, dense):
    owners = slots.shape[0]
    test, width = weighted.shape[1], modes_flat.shape[1]
    tiles = -(-block_len // 128)
    if dense:
        shape = (owners, (block_len // 128) * test + 1, 128)
    else:
        shape = (owners, test, tiles * 128)
    return pl.pallas_call(
        functools.partial(triangle_kernel, block_len, dense),
        out_shape=jax.ShapeDtypeStruct(shape, jnp.float32),
        in_specs=[pl.BlockSpec(memory_space=pltpu.SMEM)] + [pl.BlockSpec(memory_space=pltpu.VMEM)] * 3,
        out_specs=pl.BlockSpec(memory_space=pltpu.VMEM),
        scratch_shapes=[
            pltpu.VMEM((test * width, width), jnp.float32),
            pltpu.VMEM((owners if dense else 1, test, 128), jnp.float32),
        ],
    )(slots, weighted, grads, modes_flat)


def shards(modes, cell_weight, pair_owner):
    width = modes.shape[4]
    size_x = lax.axis_size("gx")
    size_y = lax.axis_size("gy")
    size_z = lax.axis_size("gz")
    owners = size_x * size_y * size_z
    grads = face_gradients(modes)
    mode_flat = modes.reshape(3, -1, width)
    grad_flat = grads.reshape(3, 3, -1, width)
    weight_flat = cell_weight.reshape(-1)
    total_cells = modes.shape[1] * modes.shape[2] * modes.shape[3] * owners
    scale = 1.0 / jnp.sqrt(jnp.float32(3.0 * total_cells))
    cells = mode_flat.shape[1]
    weighted = mode_flat[:, :, :TEST] * (weight_flat * scale)[None, :, None]
    weighted = jnp.tile(jnp.swapaxes(weighted, 1, 2), (1, 1, 3))
    grads_t = grad_flat.transpose(0, 3, 1, 2).reshape(3, width, 3 * cells)
    pair_total = width * (width + 1) // 2
    block_len = (pair_total + owners - 1) // owners
    ranks = jnp.arange(owners, dtype=jnp.int32)
    slots = jnp.sum(jnp.where(pair_owner[None, :] == ranks[:, None], ranks[None, :], 0), axis=1)
    slots = jnp.clip(slots, 0, owners - 1).astype(jnp.int32)
    full, spare = block_len // 128, block_len % 128
    dense = 0 < spare and spare * TEST <= 128
    placed = triangle(slots, weighted, grads_t, mode_flat.reshape(3 * cells, width), block_len, dense)
    if dense:
        owned = scatter_sum(placed, ("gx", "gy", "gz"))[0]
        main = owned[: full * TEST].reshape(full, TEST, 128).transpose(1, 0, 2).reshape(TEST, full * 128)
        tail = owned[full * TEST, : spare * TEST].reshape(spare, TEST).T
        return jnp.concatenate([main, tail], axis=1)
    partial_terms = placed[:, :, :block_len].reshape(owners, TEST * block_len)
    lanes = 128
    rows = -(-TEST * block_len // lanes)
    partial_terms = jnp.pad(partial_terms, ((0, 0), (0, rows * lanes - TEST * block_len)))
    owned = scatter_sum(partial_terms.reshape(owners, rows, lanes), ("gx", "gy", "gz"))
    return owned.reshape(-1)[: TEST * block_len].reshape(TEST, block_len)

def solution(mesh):
    placed = (P("groups", "gx", "gy", "gz", None), P("gx", "gy", "gz"), P())
    return jax.shard_map(
        shards,
        mesh=mesh,
        in_specs=placed,
        out_specs=P("groups", ("gx", "gy", "gz")),
        check_vma=False,
    )
```

```python
import functools

import jax
import jax.numpy as jnp
import numpy as np
from jax import lax
from jax.experimental import pallas as pl
from jax.experimental.pallas import tpu as pltpu
from jax.sharding import PartitionSpec as P

TEST = 64


def extended(value, sides, width):
    for axis, dim in sides:
        peers, length = (lax.axis_size(axis), value.shape[dim])
        up = [(i, (i + 1) % peers) for i in range(peers)]
        down = [(j, i) for i, j in up]
        last = lax.slice_in_dim(value, length - width, length, axis=dim)
        leading = lax.slice_in_dim(value, 0, width, axis=dim)
        before = lax.ppermute(last, axis, up)
        after = lax.ppermute(leading, axis, down)
        value = jnp.concatenate([before, value, after], axis=dim)
    return value


def gradients(padded):
    step_x = (padded[:, 2:, 1:-1, 1:-1] - padded[:, :-2, 1:-1, 1:-1]) * 0.5
    step_y = (padded[:, 1:-1, 2:, 1:-1] - padded[:, 1:-1, :-2, 1:-1]) * 0.5
    step_z = (padded[:, 1:-1, 1:-1, 2:] - padded[:, 1:-1, 1:-1, :-2]) * 0.5
    return jnp.stack([step_x, step_y, step_z], axis=1)


def face_gradients(value):
    steps = []
    for axis, dim in (("gx", 1), ("gy", 2), ("gz", 3)):
        peers, length = lax.axis_size(axis), value.shape[dim]
        up = [(i, (i + 1) % peers) for i in range(peers)]
        down = [(j, i) for i, j in up]
        last = lax.slice_in_dim(value, length - 1, length, axis=dim)
        leading = lax.slice_in_dim(value, 0, 1, axis=dim)
        if axis == "gz" and peers == 2:
            level = lax.axis_index(axis)
            got = lax.ppermute(jnp.where(level == 0, last, leading), axis, [(0, 1), (1, 0)])
            before = jnp.where(level == 1, got, jnp.float32(0.0))
            after = jnp.where(level == 0, got, jnp.float32(0.0))
        else:
            before = lax.ppermute(last, axis, up)
            after = lax.ppermute(leading, axis, down)
            if axis == "gz":
                level = lax.axis_index(axis)
                before = jnp.where(level == 0, jnp.float32(0.0), before)
                after = jnp.where(level == peers - 1, jnp.float32(0.0), after)
        ext = jnp.concatenate([before, value, after], axis=dim)
        high = lax.slice_in_dim(ext, 2, length + 2, axis=dim)
        low = lax.slice_in_dim(ext, 0, length, axis=dim)
        steps.append((high - low) * 0.5)
    return jnp.stack(steps, axis=1)


def halving_stages(axes):
    stages = []
    for axis in axes:
        size = lax.axis_size(axis)
        bit = size // 2
        while bit >= 1:
            stages.append((axis, bit, size))
            bit //= 2
    return stages


def halve(value, axis, bit, size, dim):
    pairs = [(i, i ^ bit) for i in range(size)]
    mine = (lax.axis_index(axis) // bit) % 2
    keep = lax.dynamic_index_in_dim(value, mine, dim, keepdims=True)
    other = lax.dynamic_index_in_dim(value, 1 - mine, dim, keepdims=True)
    return keep + lax.ppermute(other, axis, pairs)


def scatter_sum(payload, axes):
    sizes = [lax.axis_size(a) for a in axes]
    if any(s & (s - 1) for s in sizes):
        return lax.psum_scatter(payload, tuple(axes), scatter_dimension=0, tiled=True)
    stages = halving_stages(axes)
    rows, lanes = payload.shape[1], payload.shape[2]
    value = payload.reshape((2,) * len(stages) + (rows, lanes))
    first = [k for k, s in enumerate(stages) if s[0] == axes[-1]]
    for k in first:
        value = halve(value, *stages[k], k)
    rest = [k for k in range(len(stages)) if k not in first]
    tail = rest[:1] if rest and stages[rest[0]][1] > 1 else []
    head = [k for k in rest if k not in tail][::-1]
    count = min(3, len(rest), rows)
    cuts = np.array_split(np.arange(rows), count) if count else [np.arange(rows)]
    parts = []
    for p, cut in enumerate(cuts):
        part = value[..., int(cut[0]) : int(cut[-1]) + 1, :]
        turn = p % len(head) if head else 0
        for k in head[turn:] + head[:turn] + tail:
            part = halve(part, *stages[k], k)
        parts.append(part)
    value = jnp.concatenate(parts, axis=-2) if len(parts) > 1 else parts[0]
    return value.reshape(1, rows, lanes)


def triangle_kernel(block_len, dense, slot_ref, w_ref, g_ref, m_ref, out_ref, sym_ref, rest_ref):
    test, width = w_ref.shape[1], m_ref.shape[1]
    group = 16
    full = block_len // 128 if dense else out_ref.shape[2] // 128
    out_ref[...] = jnp.zeros(out_ref.shape, out_ref.dtype)
    rest_ref[...] = jnp.zeros(rest_ref.shape, rest_ref.dtype)

    def contract(step, carry):
        slabs = []
        for u in range(group):
            i = step * group + u
            zt = w_ref[0, pl.ds(i, 1), :] * g_ref[0]
            zt = zt + w_ref[1, pl.ds(i, 1), :] * g_ref[1]
            zt = zt + w_ref[2, pl.ds(i, 1), :] * g_ref[2]
            slabs.append(zt)
        zt = jnp.concatenate(slabs, axis=0)
        part = jnp.dot(zt, m_ref[...], precision=lax.Precision.HIGH, preferred_element_type=jnp.float32)
        for u in range(group):
            piece = part[u * width : (u + 1) * width, :]
            start = pl.multiple_of((step * group + u) * width, width)
            sym_ref[pl.ds(start, width), :] = piece + piece.T
        return carry

    lax.fori_loop(0, test // group, contract, 0)
    lane = lax.broadcasted_iota(jnp.int32, (test, 128), 1)
    for j in range(width):
        slab = sym_ref[pl.ds(j, test, stride=width), :]
        offset = j * width - (j * (j - 1)) // 2
        stop = offset + width - j
        for c in range(offset // block_len, (stop - 1) // block_len + 1):
            lo = max(offset, c * block_len) - c * block_len
            hi = min(stop, (c + 1) * block_len) - c * block_len
            slot = slot_ref[c]
            for u in range(lo // 128, (hi - 1) // 128 + 1):
                base = c * block_len + u * 128
                rolled = pltpu.roll(slab, (offset - j - base) % 128, 1)
                keep = (lane >= lo - u * 128) & (lane < hi - u * 128)
                if u < full and dense:
                    target = out_ref.at[slot, pl.ds(u * test, test), :]
                elif u < full:
                    target = out_ref.at[slot, :, pl.ds(u * 128, 128)]
                else:
                    target = rest_ref.at[slot]
                target[...] = jnp.where(keep, rolled, target[...])
    if dense:
        spare = block_len - full * 128
        row = lax.broadcasted_iota(jnp.int32, (test, 128), 0)
        for s in range(out_ref.shape[0]):
            tail = rest_ref[s]
            picked = jnp.zeros((test, 128), jnp.float32)
            for r in range(spare):
                hit = (lane >= r * test) & (lane < (r + 1) * test) & (lane - r * test == row)
                picked = jnp.where(hit, jnp.broadcast_to(tail[:, r : r + 1], (test, 128)), picked)
            out_ref[s, pl.ds(full * test, 1), :] = jnp.sum(picked, axis=0, keepdims=True)


def triangle(slots, weighted, grads, modes_flat, block_len, dense):
    owners = slots.shape[0]
    test, width = weighted.shape[1], modes_flat.shape[1]
    tiles = -(-block_len // 128)
    if dense:
        shape = (owners, (block_len // 128) * test + 1, 128)
    else:
        shape = (owners, test, tiles * 128)
    return pl.pallas_call(
        functools.partial(triangle_kernel, block_len, dense),
        out_shape=jax.ShapeDtypeStruct(shape, jnp.float32),
        in_specs=[pl.BlockSpec(memory_space=pltpu.SMEM)] + [pl.BlockSpec(memory_space=pltpu.VMEM)] * 3,
        out_specs=pl.BlockSpec(memory_space=pltpu.VMEM),
        scratch_shapes=[
            pltpu.VMEM((test * width, width), jnp.float32),
            pltpu.VMEM((owners if dense else 1, test, 128), jnp.float32),
        ],
    )(slots, weighted, grads, modes_flat)


def shards(modes, cell_weight, pair_owner):
    width = modes.shape[4]
    size_x = lax.axis_size("gx")
    size_y = lax.axis_size("gy")
    size_z = lax.axis_size("gz")
    owners = size_x * size_y * size_z
    grads = face_gradients(modes)
    mode_flat = modes.reshape(3, -1, width)
    grad_flat = grads.reshape(3, 3, -1, width)
    weight_flat = cell_weight.reshape(-1)
    total_cells = modes.shape[1] * modes.shape[2] * modes.shape[3] * owners
    scale = 1.0 / jnp.sqrt(jnp.float32(3.0 * total_cells))
    cells = mode_flat.shape[1]
    weighted = mode_flat[:, :, :TEST] * (weight_flat * scale)[None, :, None]
    weighted = jnp.tile(jnp.swapaxes(weighted, 1, 2), (1, 1, 3))
    grads_t = grad_flat.transpose(0, 3, 1, 2).reshape(3, width, 3 * cells)
    pair_total = width * (width + 1) // 2
    block_len = (pair_total + owners - 1) // owners
    ranks = jnp.arange(owners, dtype=jnp.int32)
    slots = jnp.sum(jnp.where(pair_owner[None, :] == ranks[:, None], ranks[None, :], 0), axis=1)
    slots = jnp.clip(slots, 0, owners - 1).astype(jnp.int32)
    full, spare = block_len // 128, block_len % 128
    dense = 0 < spare and spare * TEST <= 128
    placed = triangle(slots, weighted, grads_t, mode_flat.reshape(3 * cells, width), block_len, dense)
    if dense:
        owned = scatter_sum(placed, ("gx", "gy", "gz"))[0]
        main = owned[: full * TEST].reshape(full, TEST, 128).transpose(1, 0, 2).reshape(TEST, full * 128)
        tail = owned[full * TEST, : spare * TEST].reshape(spare, TEST).T
        return jnp.concatenate([main, tail], axis=1)
    partial_terms = placed[:, :, :block_len].reshape(owners, TEST * block_len)
    lanes = 128
    rows = -(-TEST * block_len // lanes)
    partial_terms = jnp.pad(partial_terms, ((0, 0), (0, rows * lanes - TEST * block_len)))
    owned = scatter_sum(partial_terms.reshape(owners, rows, lanes), ("gx", "gy", "gz"))
    return owned.reshape(-1)[: TEST * block_len].reshape(TEST, block_len)

def solution(mesh):
    placed = (P("groups", "gx", "gy", "gz", None), P("gx", "gy", "gz"), P())
    return jax.shard_map(
        shards,
        mesh=mesh,
        in_specs=placed,
        out_specs=P("groups", ("gx", "gy", "gz")),
        check_vma=False,
    )
```

```python
import functools

import jax
import jax.numpy as jnp
import numpy as np
from jax import lax
from jax.experimental import pallas as pl
from jax.experimental.pallas import tpu as pltpu
from jax.sharding import PartitionSpec as P

TEST = 64


def extended(value, sides, width):
    for axis, dim in sides:
        peers, length = (lax.axis_size(axis), value.shape[dim])
        up = [(i, (i + 1) % peers) for i in range(peers)]
        down = [(j, i) for i, j in up]
        last = lax.slice_in_dim(value, length - width, length, axis=dim)
        leading = lax.slice_in_dim(value, 0, width, axis=dim)
        before = lax.ppermute(last, axis, up)
        after = lax.ppermute(leading, axis, down)
        value = jnp.concatenate([before, value, after], axis=dim)
    return value


def gradients(padded):
    step_x = (padded[:, 2:, 1:-1, 1:-1] - padded[:, :-2, 1:-1, 1:-1]) * 0.5
    step_y = (padded[:, 1:-1, 2:, 1:-1] - padded[:, 1:-1, :-2, 1:-1]) * 0.5
    step_z = (padded[:, 1:-1, 1:-1, 2:] - padded[:, 1:-1, 1:-1, :-2]) * 0.5
    return jnp.stack([step_x, step_y, step_z], axis=1)


def face_gradients(value):
    steps = []
    for axis, dim in (("gx", 1), ("gy", 2), ("gz", 3)):
        peers, length = lax.axis_size(axis), value.shape[dim]
        up = [(i, (i + 1) % peers) for i in range(peers)]
        down = [(j, i) for i, j in up]
        last = lax.slice_in_dim(value, length - 1, length, axis=dim)
        leading = lax.slice_in_dim(value, 0, 1, axis=dim)
        if axis == "gz" and peers == 2:
            level = lax.axis_index(axis)
            got = lax.ppermute(jnp.where(level == 0, last, leading), axis, [(0, 1), (1, 0)])
            before = jnp.where(level == 1, got, jnp.float32(0.0))
            after = jnp.where(level == 0, got, jnp.float32(0.0))
        else:
            before = lax.ppermute(last, axis, up)
            after = lax.ppermute(leading, axis, down)
            if axis == "gz":
                level = lax.axis_index(axis)
                before = jnp.where(level == 0, jnp.float32(0.0), before)
                after = jnp.where(level == peers - 1, jnp.float32(0.0), after)
        ext = jnp.concatenate([before, value, after], axis=dim)
        high = lax.slice_in_dim(ext, 2, length + 2, axis=dim)
        low = lax.slice_in_dim(ext, 0, length, axis=dim)
        steps.append((high - low) * 0.5)
    return jnp.stack(steps, axis=1)


def halving_stages(axes):
    stages = []
    for axis in axes:
        size = lax.axis_size(axis)
        bit = size // 2
        while bit >= 1:
            stages.append((axis, bit, size))
            bit //= 2
    return stages


def halve(value, axis, bit, size, dim):
    pairs = [(i, i ^ bit) for i in range(size)]
    mine = (lax.axis_index(axis) // bit) % 2
    keep = lax.dynamic_index_in_dim(value, mine, dim, keepdims=True)
    other = lax.dynamic_index_in_dim(value, 1 - mine, dim, keepdims=True)
    return keep + lax.ppermute(other, axis, pairs)


def scatter_sum(payload, axes):
    sizes = [lax.axis_size(a) for a in axes]
    if any(s & (s - 1) for s in sizes):
        return lax.psum_scatter(payload, tuple(axes), scatter_dimension=0, tiled=True)
    stages = halving_stages(axes)
    rows, lanes = payload.shape[1], payload.shape[2]
    value = payload.reshape((2,) * len(stages) + (rows, lanes))
    first = [k for k, s in enumerate(stages) if s[0] == axes[-1]]
    for k in first:
        value = halve(value, *stages[k], k)
    rest = [k for k in range(len(stages)) if k not in first]
    tail = rest[:1] if rest and stages[rest[0]][1] > 1 else []
    head = [k for k in rest if k not in tail][::-1]
    count = min(3, len(rest), rows)
    cuts = np.array_split(np.arange(rows), count) if count else [np.arange(rows)]
    parts = []
    for p, cut in enumerate(cuts):
        part = value[..., int(cut[0]) : int(cut[-1]) + 1, :]
        turn = p % len(head) if head else 0
        for k in head[turn:] + head[:turn] + tail:
            part = halve(part, *stages[k], k)
        parts.append(part)
    value = jnp.concatenate(parts, axis=-2) if len(parts) > 1 else parts[0]
    return value.reshape(1, rows, lanes)


def triangle_kernel(block_len, dense, slot_ref, w_ref, g_ref, m_ref, out_ref, sym_ref, rest_ref):
    test, width = w_ref.shape[1], m_ref.shape[1]
    group = 32
    full = block_len // 128 if dense else out_ref.shape[2] // 128
    out_ref[...] = jnp.zeros(out_ref.shape, out_ref.dtype)
    rest_ref[...] = jnp.zeros(rest_ref.shape, rest_ref.dtype)

    def contract(step, carry):
        slabs = []
        for u in range(group):
            i = step * group + u
            zt = w_ref[0, pl.ds(i, 1), :] * g_ref[0]
            zt = zt + w_ref[1, pl.ds(i, 1), :] * g_ref[1]
            zt = zt + w_ref[2, pl.ds(i, 1), :] * g_ref[2]
            slabs.append(zt)
        zt = jnp.concatenate(slabs, axis=0)
        part = jnp.dot(zt, m_ref[...], precision=lax.Precision.HIGH, preferred_element_type=jnp.float32)
        for u in range(group):
            piece = part[u * width : (u + 1) * width, :]
            start = pl.multiple_of((step * group + u) * width, width)
            sym_ref[pl.ds(start, width), :] = piece + piece.T
        return carry

    lax.fori_loop(0, test // group, contract, 0)
    lane = lax.broadcasted_iota(jnp.int32, (test, 128), 1)
    for j in range(width):
        slab = sym_ref[pl.ds(j, test, stride=width), :]
        offset = j * width - (j * (j - 1)) // 2
        stop = offset + width - j
        for c in range(offset // block_len, (stop - 1) // block_len + 1):
            lo = max(offset, c * block_len) - c * block_len
            hi = min(stop, (c + 1) * block_len) - c * block_len
            slot = slot_ref[c]
            for u in range(lo // 128, (hi - 1) // 128 + 1):
                base = c * block_len + u * 128
                rolled = pltpu.roll(slab, (offset - j - base) % 128, 1)
                keep = (lane >= lo - u * 128) & (lane < hi - u * 128)
                if u < full and dense:
                    target = out_ref.at[slot, pl.ds(u * test, test), :]
                elif u < full:
                    target = out_ref.at[slot, :, pl.ds(u * 128, 128)]
                else:
                    target = rest_ref.at[slot]
                target[...] = jnp.where(keep, rolled, target[...])
    if dense:
        spare = block_len - full * 128
        row = lax.broadcasted_iota(jnp.int32, (test, 128), 0)
        for s in range(out_ref.shape[0]):
            tail = rest_ref[s]
            picked = jnp.zeros((test, 128), jnp.float32)
            for r in range(spare):
                hit = (lane >= r * test) & (lane < (r + 1) * test) & (lane - r * test == row)
                picked = jnp.where(hit, jnp.broadcast_to(tail[:, r : r + 1], (test, 128)), picked)
            out_ref[s, pl.ds(full * test, 1), :] = jnp.sum(picked, axis=0, keepdims=True)


def triangle(slots, weighted, grads, modes_flat, block_len, dense):
    owners = slots.shape[0]
    test, width = weighted.shape[1], modes_flat.shape[1]
    tiles = -(-block_len // 128)
    if dense:
        shape = (owners, (block_len // 128) * test + 1, 128)
    else:
        shape = (owners, test, tiles * 128)
    return pl.pallas_call(
        functools.partial(triangle_kernel, block_len, dense),
        out_shape=jax.ShapeDtypeStruct(shape, jnp.float32),
        in_specs=[pl.BlockSpec(memory_space=pltpu.SMEM)] + [pl.BlockSpec(memory_space=pltpu.VMEM)] * 3,
        out_specs=pl.BlockSpec(memory_space=pltpu.VMEM),
        scratch_shapes=[
            pltpu.VMEM((test * width, width), jnp.float32),
            pltpu.VMEM((owners if dense else 1, test, 128), jnp.float32),
        ],
    )(slots, weighted, grads, modes_flat)


def shards(modes, cell_weight, pair_owner):
    width = modes.shape[4]
    size_x = lax.axis_size("gx")
    size_y = lax.axis_size("gy")
    size_z = lax.axis_size("gz")
    owners = size_x * size_y * size_z
    grads = face_gradients(modes)
    mode_flat = modes.reshape(3, -1, width)
    grad_flat = grads.reshape(3, 3, -1, width)
    weight_flat = cell_weight.reshape(-1)
    total_cells = modes.shape[1] * modes.shape[2] * modes.shape[3] * owners
    scale = 1.0 / jnp.sqrt(jnp.float32(3.0 * total_cells))
    cells = mode_flat.shape[1]
    weighted = mode_flat[:, :, :TEST] * (weight_flat * scale)[None, :, None]
    weighted = jnp.tile(jnp.swapaxes(weighted, 1, 2), (1, 1, 3))
    grads_t = grad_flat.transpose(0, 3, 1, 2).reshape(3, width, 3 * cells)
    pair_total = width * (width + 1) // 2
    block_len = (pair_total + owners - 1) // owners
    ranks = jnp.arange(owners, dtype=jnp.int32)
    slots = jnp.sum(jnp.where(pair_owner[None, :] == ranks[:, None], ranks[None, :], 0), axis=1)
    slots = jnp.clip(slots, 0, owners - 1).astype(jnp.int32)
    full, spare = block_len // 128, block_len % 128
    dense = 0 < spare and spare * TEST <= 128
    placed = triangle(slots, weighted, grads_t, mode_flat.reshape(3 * cells, width), block_len, dense)
    if dense:
        owned = scatter_sum(placed, ("gx", "gy", "gz"))[0]
        main = owned[: full * TEST].reshape(full, TEST, 128).transpose(1, 0, 2).reshape(TEST, full * 128)
        tail = owned[full * TEST, : spare * TEST].reshape(spare, TEST).T
        return jnp.concatenate([main, tail], axis=1)
    partial_terms = placed[:, :, :block_len].reshape(owners, TEST * block_len)
    lanes = 128
    rows = -(-TEST * block_len // lanes)
    partial_terms = jnp.pad(partial_terms, ((0, 0), (0, rows * lanes - TEST * block_len)))
    owned = scatter_sum(partial_terms.reshape(owners, rows, lanes), ("gx", "gy", "gz"))
    return owned.reshape(-1)[: TEST * block_len].reshape(TEST, block_len)

def solution(mesh):
    placed = (P("groups", "gx", "gy", "gz", None), P("gx", "gy", "gz"), P())
    return jax.shard_map(
        shards,
        mesh=mesh,
        in_specs=placed,
        out_specs=P("groups", ("gx", "gy", "gz")),
        check_vma=False,
    )
```

```python
import functools

import jax
import jax.numpy as jnp
import numpy as np
from jax import lax
from jax.experimental import pallas as pl
from jax.experimental.pallas import tpu as pltpu
from jax.sharding import PartitionSpec as P

TEST = 64


def extended(value, sides, width):
    for axis, dim in sides:
        peers, length = (lax.axis_size(axis), value.shape[dim])
        up = [(i, (i + 1) % peers) for i in range(peers)]
        down = [(j, i) for i, j in up]
        last = lax.slice_in_dim(value, length - width, length, axis=dim)
        leading = lax.slice_in_dim(value, 0, width, axis=dim)
        before = lax.ppermute(last, axis, up)
        after = lax.ppermute(leading, axis, down)
        value = jnp.concatenate([before, value, after], axis=dim)
    return value


def gradients(padded):
    step_x = (padded[:, 2:, 1:-1, 1:-1] - padded[:, :-2, 1:-1, 1:-1]) * 0.5
    step_y = (padded[:, 1:-1, 2:, 1:-1] - padded[:, 1:-1, :-2, 1:-1]) * 0.5
    step_z = (padded[:, 1:-1, 1:-1, 2:] - padded[:, 1:-1, 1:-1, :-2]) * 0.5
    return jnp.stack([step_x, step_y, step_z], axis=1)


def face_gradients(value):
    steps = []
    for axis, dim in (("gx", 1), ("gy", 2), ("gz", 3)):
        peers, length = lax.axis_size(axis), value.shape[dim]
        up = [(i, (i + 1) % peers) for i in range(peers)]
        down = [(j, i) for i, j in up]
        last = lax.slice_in_dim(value, length - 1, length, axis=dim)
        leading = lax.slice_in_dim(value, 0, 1, axis=dim)
        if axis == "gz" and peers == 2:
            level = lax.axis_index(axis)
            got = lax.ppermute(jnp.where(level == 0, last, leading), axis, [(0, 1), (1, 0)])
            before = jnp.where(level == 1, got, jnp.float32(0.0))
            after = jnp.where(level == 0, got, jnp.float32(0.0))
        else:
            before = lax.ppermute(last, axis, up)
            after = lax.ppermute(leading, axis, down)
            if axis == "gz":
                level = lax.axis_index(axis)
                before = jnp.where(level == 0, jnp.float32(0.0), before)
                after = jnp.where(level == peers - 1, jnp.float32(0.0), after)
        ext = jnp.concatenate([before, value, after], axis=dim)
        high = lax.slice_in_dim(ext, 2, length + 2, axis=dim)
        low = lax.slice_in_dim(ext, 0, length, axis=dim)
        steps.append((high - low) * 0.5)
    return jnp.stack(steps, axis=1)


def halving_stages(axes):
    stages = []
    for axis in axes:
        size = lax.axis_size(axis)
        bit = size // 2
        while bit >= 1:
            stages.append((axis, bit, size))
            bit //= 2
    return stages


def halve(value, axis, bit, size, dim):
    pairs = [(i, i ^ bit) for i in range(size)]
    mine = (lax.axis_index(axis) // bit) % 2
    keep = lax.dynamic_index_in_dim(value, mine, dim, keepdims=True)
    other = lax.dynamic_index_in_dim(value, 1 - mine, dim, keepdims=True)
    return keep + lax.ppermute(other, axis, pairs)


def scatter_sum(payload, axes):
    sizes = [lax.axis_size(a) for a in axes]
    if any(s & (s - 1) for s in sizes):
        return lax.psum_scatter(payload, tuple(axes), scatter_dimension=0, tiled=True)
    stages = halving_stages(axes)
    rows, lanes = payload.shape[1], payload.shape[2]
    value = payload.reshape((2,) * len(stages) + (rows, lanes))
    first = [k for k, s in enumerate(stages) if s[0] == axes[-1]]
    for k in first:
        value = halve(value, *stages[k], k)
    rest = [k for k in range(len(stages)) if k not in first]
    tail = rest[:1] if rest and stages[rest[0]][1] > 1 else []
    head = [k for k in rest if k not in tail][::-1]
    count = min(3, len(rest), rows)
    cuts = np.array_split(np.arange(rows), count) if count else [np.arange(rows)]
    parts = []
    for p, cut in enumerate(cuts):
        part = value[..., int(cut[0]) : int(cut[-1]) + 1, :]
        turn = p % len(head) if head else 0
        for k in head[turn:] + head[:turn] + tail:
            part = halve(part, *stages[k], k)
        parts.append(part)
    value = jnp.concatenate(parts, axis=-2) if len(parts) > 1 else parts[0]
    return value.reshape(1, rows, lanes)


def triangle_kernel(block_len, dense, slot_ref, w_ref, g_ref, m_ref, out_ref, sym_ref, rest_ref):
    test, width = w_ref.shape[1], m_ref.shape[1]
    group = 64
    full = block_len // 128 if dense else out_ref.shape[2] // 128
    out_ref[...] = jnp.zeros(out_ref.shape, out_ref.dtype)
    rest_ref[...] = jnp.zeros(rest_ref.shape, rest_ref.dtype)

    def contract(step, carry):
        slabs = []
        for u in range(group):
            i = step * group + u
            zt = w_ref[0, pl.ds(i, 1), :] * g_ref[0]
            zt = zt + w_ref[1, pl.ds(i, 1), :] * g_ref[1]
            zt = zt + w_ref[2, pl.ds(i, 1), :] * g_ref[2]
            slabs.append(zt)
        zt = jnp.concatenate(slabs, axis=0)
        part = jnp.dot(zt, m_ref[...], precision=lax.Precision.HIGH, preferred_element_type=jnp.float32)
        for u in range(group):
            piece = part[u * width : (u + 1) * width, :]
            start = pl.multiple_of((step * group + u) * width, width)
            sym_ref[pl.ds(start, width), :] = piece + piece.T
        return carry

    lax.fori_loop(0, test // group, contract, 0)
    lane = lax.broadcasted_iota(jnp.int32, (test, 128), 1)
    for j in range(width):
        slab = sym_ref[pl.ds(j, test, stride=width), :]
        offset = j * width - (j * (j - 1)) // 2
        stop = offset + width - j
        for c in range(offset // block_len, (stop - 1) // block_len + 1):
            lo = max(offset, c * block_len) - c * block_len
            hi = min(stop, (c + 1) * block_len) - c * block_len
            slot = slot_ref[c]
            for u in range(lo // 128, (hi - 1) // 128 + 1):
                base = c * block_len + u * 128
                rolled = pltpu.roll(slab, (offset - j - base) % 128, 1)
                keep = (lane >= lo - u * 128) & (lane < hi - u * 128)
                if u < full and dense:
                    target = out_ref.at[slot, pl.ds(u * test, test), :]
                elif u < full:
                    target = out_ref.at[slot, :, pl.ds(u * 128, 128)]
                else:
                    target = rest_ref.at[slot]
                target[...] = jnp.where(keep, rolled, target[...])
    if dense:
        spare = block_len - full * 128
        row = lax.broadcasted_iota(jnp.int32, (test, 128), 0)
        for s in range(out_ref.shape[0]):
            tail = rest_ref[s]
            picked = jnp.zeros((test, 128), jnp.float32)
            for r in range(spare):
                hit = (lane >= r * test) & (lane < (r + 1) * test) & (lane - r * test == row)
                picked = jnp.where(hit, jnp.broadcast_to(tail[:, r : r + 1], (test, 128)), picked)
            out_ref[s, pl.ds(full * test, 1), :] = jnp.sum(picked, axis=0, keepdims=True)


def triangle(slots, weighted, grads, modes_flat, block_len, dense):
    owners = slots.shape[0]
    test, width = weighted.shape[1], modes_flat.shape[1]
    tiles = -(-block_len // 128)
    if dense:
        shape = (owners, (block_len // 128) * test + 1, 128)
    else:
        shape = (owners, test, tiles * 128)
    return pl.pallas_call(
        functools.partial(triangle_kernel, block_len, dense),
        out_shape=jax.ShapeDtypeStruct(shape, jnp.float32),
        in_specs=[pl.BlockSpec(memory_space=pltpu.SMEM)] + [pl.BlockSpec(memory_space=pltpu.VMEM)] * 3,
        out_specs=pl.BlockSpec(memory_space=pltpu.VMEM),
        scratch_shapes=[
            pltpu.VMEM((test * width, width), jnp.float32),
            pltpu.VMEM((owners if dense else 1, test, 128), jnp.float32),
        ],
    )(slots, weighted, grads, modes_flat)


def shards(modes, cell_weight, pair_owner):
    width = modes.shape[4]
    size_x = lax.axis_size("gx")
    size_y = lax.axis_size("gy")
    size_z = lax.axis_size("gz")
    owners = size_x * size_y * size_z
    grads = face_gradients(modes)
    mode_flat = modes.reshape(3, -1, width)
    grad_flat = grads.reshape(3, 3, -1, width)
    weight_flat = cell_weight.reshape(-1)
    total_cells = modes.shape[1] * modes.shape[2] * modes.shape[3] * owners
    scale = 1.0 / jnp.sqrt(jnp.float32(3.0 * total_cells))
    cells = mode_flat.shape[1]
    weighted = mode_flat[:, :, :TEST] * (weight_flat * scale)[None, :, None]
    weighted = jnp.tile(jnp.swapaxes(weighted, 1, 2), (1, 1, 3))
    grads_t = grad_flat.transpose(0, 3, 1, 2).reshape(3, width, 3 * cells)
    pair_total = width * (width + 1) // 2
    block_len = (pair_total + owners - 1) // owners
    ranks = jnp.arange(owners, dtype=jnp.int32)
    slots = jnp.sum(jnp.where(pair_owner[None, :] == ranks[:, None], ranks[None, :], 0), axis=1)
    slots = jnp.clip(slots, 0, owners - 1).astype(jnp.int32)
    full, spare = block_len // 128, block_len % 128
    dense = 0 < spare and spare * TEST <= 128
    placed = triangle(slots, weighted, grads_t, mode_flat.reshape(3 * cells, width), block_len, dense)
    if dense:
        owned = scatter_sum(placed, ("gx", "gy", "gz"))[0]
        main = owned[: full * TEST].reshape(full, TEST, 128).transpose(1, 0, 2).reshape(TEST, full * 128)
        tail = owned[full * TEST, : spare * TEST].reshape(spare, TEST).T
        return jnp.concatenate([main, tail], axis=1)
    partial_terms = placed[:, :, :block_len].reshape(owners, TEST * block_len)
    lanes = 128
    rows = -(-TEST * block_len // lanes)
    partial_terms = jnp.pad(partial_terms, ((0, 0), (0, rows * lanes - TEST * block_len)))
    owned = scatter_sum(partial_terms.reshape(owners, rows, lanes), ("gx", "gy", "gz"))
    return owned.reshape(-1)[: TEST * block_len].reshape(TEST, block_len)

def solution(mesh):
    placed = (P("groups", "gx", "gy", "gz", None), P("gx", "gy", "gz"), P())
    return jax.shard_map(
        shards,
        mesh=mesh,
        in_specs=placed,
        out_specs=P("groups", ("gx", "gy", "gz")),
        check_vma=False,
    )
```

```python
import functools

import jax
import jax.numpy as jnp
import numpy as np
from jax import lax
from jax.experimental import pallas as pl
from jax.experimental.pallas import tpu as pltpu
from jax.sharding import PartitionSpec as P

TEST = 64


def extended(value, sides, width):
    for axis, dim in sides:
        peers, length = (lax.axis_size(axis), value.shape[dim])
        up = [(i, (i + 1) % peers) for i in range(peers)]
        down = [(j, i) for i, j in up]
        last = lax.slice_in_dim(value, length - width, length, axis=dim)
        leading = lax.slice_in_dim(value, 0, width, axis=dim)
        before = lax.ppermute(last, axis, up)
        after = lax.ppermute(leading, axis, down)
        value = jnp.concatenate([before, value, after], axis=dim)
    return value


def gradients(padded):
    step_x = (padded[:, 2:, 1:-1, 1:-1] - padded[:, :-2, 1:-1, 1:-1]) * 0.5
    step_y = (padded[:, 1:-1, 2:, 1:-1] - padded[:, 1:-1, :-2, 1:-1]) * 0.5
    step_z = (padded[:, 1:-1, 1:-1, 2:] - padded[:, 1:-1, 1:-1, :-2]) * 0.5
    return jnp.stack([step_x, step_y, step_z], axis=1)


def face_gradients(value):
    steps = []
    for axis, dim in (("gx", 1), ("gy", 2), ("gz", 3)):
        peers, length = lax.axis_size(axis), value.shape[dim]
        up = [(i, (i + 1) % peers) for i in range(peers)]
        down = [(j, i) for i, j in up]
        last = lax.slice_in_dim(value, length - 1, length, axis=dim)
        leading = lax.slice_in_dim(value, 0, 1, axis=dim)
        if axis == "gz" and peers == 2:
            level = lax.axis_index(axis)
            got = lax.ppermute(jnp.where(level == 0, last, leading), axis, [(0, 1), (1, 0)])
            before = jnp.where(level == 1, got, jnp.float32(0.0))
            after = jnp.where(level == 0, got, jnp.float32(0.0))
        else:
            before = lax.ppermute(last, axis, up)
            after = lax.ppermute(leading, axis, down)
            if axis == "gz":
                level = lax.axis_index(axis)
                before = jnp.where(level == 0, jnp.float32(0.0), before)
                after = jnp.where(level == peers - 1, jnp.float32(0.0), after)
        ext = jnp.concatenate([before, value, after], axis=dim)
        high = lax.slice_in_dim(ext, 2, length + 2, axis=dim)
        low = lax.slice_in_dim(ext, 0, length, axis=dim)
        steps.append((high - low) * 0.5)
    return jnp.stack(steps, axis=1)


def halving_stages(axes):
    stages = []
    for axis in axes:
        size = lax.axis_size(axis)
        bit = size // 2
        while bit >= 1:
            stages.append((axis, bit, size))
            bit //= 2
    return stages


def halve(value, axis, bit, size, dim):
    pairs = [(i, i ^ bit) for i in range(size)]
    mine = (lax.axis_index(axis) // bit) % 2
    keep = lax.dynamic_index_in_dim(value, mine, dim, keepdims=True)
    other = lax.dynamic_index_in_dim(value, 1 - mine, dim, keepdims=True)
    return keep + lax.ppermute(other, axis, pairs)


def scatter_sum(payload, axes):
    sizes = [lax.axis_size(a) for a in axes]
    if any(s & (s - 1) for s in sizes):
        return lax.psum_scatter(payload, tuple(axes), scatter_dimension=0, tiled=True)
    stages = halving_stages(axes)
    rows, lanes = payload.shape[1], payload.shape[2]
    value = payload.reshape((2,) * len(stages) + (rows, lanes))
    first = [k for k, s in enumerate(stages) if s[0] == axes[-1]]
    for k in first:
        value = halve(value, *stages[k], k)
    rest = [k for k in range(len(stages)) if k not in first]
    tail = rest[:1] if rest and stages[rest[0]][1] > 1 else []
    head = [k for k in rest if k not in tail][::-1]
    count = min(3, len(rest), rows)
    cuts = np.array_split(np.arange(rows), count) if count else [np.arange(rows)]
    parts = []
    for p, cut in enumerate(cuts):
        part = value[..., int(cut[0]) : int(cut[-1]) + 1, :]
        turn = p % len(head) if head else 0
        for k in head[turn:] + head[:turn] + tail:
            part = halve(part, *stages[k], k)
        parts.append(part)
    value = jnp.concatenate(parts, axis=-2) if len(parts) > 1 else parts[0]
    return value.reshape(1, rows, lanes)


def triangle_kernel(block_len, dense, slot_ref, w_ref, grad_ref, m_ref, out_ref, sym_ref, rest_ref, g_ref):
    test, width = w_ref.shape[1], m_ref.shape[1]
    cells = grad_ref.shape[2]
    for a in range(3):
        for b in range(3):
            g_ref[a, :, pl.ds(b * cells, cells)] = grad_ref[a, b].T
    group = 32
    full = block_len // 128 if dense else out_ref.shape[2] // 128
    out_ref[...] = jnp.zeros(out_ref.shape, out_ref.dtype)
    rest_ref[...] = jnp.zeros(rest_ref.shape, rest_ref.dtype)

    def contract(step, carry):
        slabs = []
        for u in range(group):
            i = step * group + u
            zt = w_ref[0, pl.ds(i, 1), :] * g_ref[0]
            zt = zt + w_ref[1, pl.ds(i, 1), :] * g_ref[1]
            zt = zt + w_ref[2, pl.ds(i, 1), :] * g_ref[2]
            slabs.append(zt)
        zt = jnp.concatenate(slabs, axis=0)
        part = jnp.dot(zt, m_ref[...], precision=lax.Precision.HIGH, preferred_element_type=jnp.float32)
        for u in range(group):
            piece = part[u * width : (u + 1) * width, :]
            start = pl.multiple_of((step * group + u) * width, width)
            sym_ref[pl.ds(start, width), :] = piece + piece.T
        return carry

    lax.fori_loop(0, test // group, contract, 0)
    lane = lax.broadcasted_iota(jnp.int32, (test, 128), 1)
    for j in range(width):
        slab = sym_ref[pl.ds(j, test, stride=width), :]
        offset = j * width - (j * (j - 1)) // 2
        stop = offset + width - j
        for c in range(offset // block_len, (stop - 1) // block_len + 1):
            lo = max(offset, c * block_len) - c * block_len
            hi = min(stop, (c + 1) * block_len) - c * block_len
            slot = slot_ref[c]
            for u in range(lo // 128, (hi - 1) // 128 + 1):
                base = c * block_len + u * 128
                rolled = pltpu.roll(slab, (offset - j - base) % 128, 1)
                keep = (lane >= lo - u * 128) & (lane < hi - u * 128)
                if u < full and dense:
                    target = out_ref.at[slot, pl.ds(u * test, test), :]
                elif u < full:
                    target = out_ref.at[slot, :, pl.ds(u * 128, 128)]
                else:
                    target = rest_ref.at[slot]
                target[...] = jnp.where(keep, rolled, target[...])
    if dense:
        spare = block_len - full * 128
        row = lax.broadcasted_iota(jnp.int32, (test, 128), 0)
        for s in range(out_ref.shape[0]):
            tail = rest_ref[s]
            picked = jnp.zeros((test, 128), jnp.float32)
            for r in range(spare):
                hit = (lane >= r * test) & (lane < (r + 1) * test) & (lane - r * test == row)
                picked = jnp.where(hit, jnp.broadcast_to(tail[:, r : r + 1], (test, 128)), picked)
            out_ref[s, pl.ds(full * test, 1), :] = jnp.sum(picked, axis=0, keepdims=True)


def triangle(slots, weighted, grads, modes_flat, block_len, dense):
    owners = slots.shape[0]
    test, width = weighted.shape[1], modes_flat.shape[1]
    tiles = -(-block_len // 128)
    if dense:
        shape = (owners, (block_len // 128) * test + 1, 128)
    else:
        shape = (owners, test, tiles * 128)
    return pl.pallas_call(
        functools.partial(triangle_kernel, block_len, dense),
        out_shape=jax.ShapeDtypeStruct(shape, jnp.float32),
        in_specs=[pl.BlockSpec(memory_space=pltpu.SMEM)] + [pl.BlockSpec(memory_space=pltpu.VMEM)] * 3,
        out_specs=pl.BlockSpec(memory_space=pltpu.VMEM),
        scratch_shapes=[
            pltpu.VMEM((test * width, width), jnp.float32),
            pltpu.VMEM((owners if dense else 1, test, 128), jnp.float32),
            pltpu.VMEM((3, width, 3 * grads.shape[2]), jnp.float32),
        ],
    )(slots, weighted, grads, modes_flat)


def shards(modes, cell_weight, pair_owner):
    width = modes.shape[4]
    size_x = lax.axis_size("gx")
    size_y = lax.axis_size("gy")
    size_z = lax.axis_size("gz")
    owners = size_x * size_y * size_z
    grads = face_gradients(modes)
    mode_flat = modes.reshape(3, -1, width)
    grad_flat = grads.reshape(3, 3, -1, width)
    weight_flat = cell_weight.reshape(-1)
    total_cells = modes.shape[1] * modes.shape[2] * modes.shape[3] * owners
    scale = 1.0 / jnp.sqrt(jnp.float32(3.0 * total_cells))
    cells = mode_flat.shape[1]
    weighted = mode_flat[:, :, :TEST] * (weight_flat * scale)[None, :, None]
    weighted = jnp.tile(jnp.swapaxes(weighted, 1, 2), (1, 1, 3))
    pair_total = width * (width + 1) // 2
    block_len = (pair_total + owners - 1) // owners
    ranks = jnp.arange(owners, dtype=jnp.int32)
    slots = jnp.sum(jnp.where(pair_owner[None, :] == ranks[:, None], ranks[None, :], 0), axis=1)
    slots = jnp.clip(slots, 0, owners - 1).astype(jnp.int32)
    full, spare = block_len // 128, block_len % 128
    dense = 0 < spare and spare * TEST <= 128
    placed = triangle(slots, weighted, grad_flat, mode_flat.reshape(3 * cells, width), block_len, dense)
    if dense:
        owned = scatter_sum(placed, ("gx", "gy", "gz"))[0]
        main = owned[: full * TEST].reshape(full, TEST, 128).transpose(1, 0, 2).reshape(TEST, full * 128)
        tail = owned[full * TEST, : spare * TEST].reshape(spare, TEST).T
        return jnp.concatenate([main, tail], axis=1)
    partial_terms = placed[:, :, :block_len].reshape(owners, TEST * block_len)
    lanes = 128
    rows = -(-TEST * block_len // lanes)
    partial_terms = jnp.pad(partial_terms, ((0, 0), (0, rows * lanes - TEST * block_len)))
    owned = scatter_sum(partial_terms.reshape(owners, rows, lanes), ("gx", "gy", "gz"))
    return owned.reshape(-1)[: TEST * block_len].reshape(TEST, block_len)

def solution(mesh):
    placed = (P("groups", "gx", "gy", "gz", None), P("gx", "gy", "gz"), P())
    return jax.shard_map(
        shards,
        mesh=mesh,
        in_specs=placed,
        out_specs=P("groups", ("gx", "gy", "gz")),
        check_vma=False,
    )
```

```python
import functools

import jax
import jax.numpy as jnp
import numpy as np
from jax import lax
from jax.experimental import pallas as pl
from jax.experimental.pallas import tpu as pltpu
from jax.sharding import PartitionSpec as P

TEST = 64


def extended(value, sides, width):
    for axis, dim in sides:
        peers, length = (lax.axis_size(axis), value.shape[dim])
        up = [(i, (i + 1) % peers) for i in range(peers)]
        down = [(j, i) for i, j in up]
        last = lax.slice_in_dim(value, length - width, length, axis=dim)
        leading = lax.slice_in_dim(value, 0, width, axis=dim)
        before = lax.ppermute(last, axis, up)
        after = lax.ppermute(leading, axis, down)
        value = jnp.concatenate([before, value, after], axis=dim)
    return value


def gradients(padded):
    step_x = (padded[:, 2:, 1:-1, 1:-1] - padded[:, :-2, 1:-1, 1:-1]) * 0.5
    step_y = (padded[:, 1:-1, 2:, 1:-1] - padded[:, 1:-1, :-2, 1:-1]) * 0.5
    step_z = (padded[:, 1:-1, 1:-1, 2:] - padded[:, 1:-1, 1:-1, :-2]) * 0.5
    return jnp.stack([step_x, step_y, step_z], axis=1)


def face_gradients(value):
    steps = []
    for axis, dim in (("gx", 1), ("gy", 2), ("gz", 3)):
        peers, length = lax.axis_size(axis), value.shape[dim]
        up = [(i, (i + 1) % peers) for i in range(peers)]
        down = [(j, i) for i, j in up]
        last = lax.slice_in_dim(value, length - 1, length, axis=dim)
        leading = lax.slice_in_dim(value, 0, 1, axis=dim)
        if axis == "gz" and peers == 2:
            level = lax.axis_index(axis)
            got = lax.ppermute(jnp.where(level == 0, last, leading), axis, [(0, 1), (1, 0)])
            before = jnp.where(level == 1, got, jnp.float32(0.0))
            after = jnp.where(level == 0, got, jnp.float32(0.0))
        else:
            before = lax.ppermute(last, axis, up)
            after = lax.ppermute(leading, axis, down)
            if axis == "gz":
                level = lax.axis_index(axis)
                before = jnp.where(level == 0, jnp.float32(0.0), before)
                after = jnp.where(level == peers - 1, jnp.float32(0.0), after)
        ext = jnp.concatenate([before, value, after], axis=dim)
        high = lax.slice_in_dim(ext, 2, length + 2, axis=dim)
        low = lax.slice_in_dim(ext, 0, length, axis=dim)
        steps.append((high - low) * 0.5)
    return jnp.stack(steps, axis=1)


def halving_stages(axes):
    stages = []
    for axis in axes:
        size = lax.axis_size(axis)
        bit = size // 2
        while bit >= 1:
            stages.append((axis, bit, size))
            bit //= 2
    return stages


def halve(value, axis, bit, size, dim):
    pairs = [(i, i ^ bit) for i in range(size)]
    mine = (lax.axis_index(axis) // bit) % 2
    keep = lax.dynamic_index_in_dim(value, mine, dim, keepdims=True)
    other = lax.dynamic_index_in_dim(value, 1 - mine, dim, keepdims=True)
    return keep + lax.ppermute(other, axis, pairs)


def scatter_sum(payload, axes, local=True):
    sizes = [lax.axis_size(a) for a in axes]
    if any(s & (s - 1) for s in sizes):
        return lax.psum_scatter(payload, tuple(axes), scatter_dimension=0, tiled=True)
    stages = halving_stages(axes)
    rows, lanes = payload.shape[1], payload.shape[2]
    value = payload.reshape((2,) * len(stages) + (rows, lanes))
    first = [k for k, s in enumerate(stages) if local and s[0] == axes[-1]]
    for k in first:
        value = halve(value, *stages[k], k)
    rest = [k for k in range(len(stages)) if k not in first]
    tail = rest[:1] if rest and stages[rest[0]][1] > 1 else []
    head = [k for k in rest if k not in tail][::-1]
    count = min(3, len(rest), rows)
    cuts = np.array_split(np.arange(rows), count) if count else [np.arange(rows)]
    parts = []
    for p, cut in enumerate(cuts):
        part = value[..., int(cut[0]) : int(cut[-1]) + 1, :]
        turn = p % len(head) if head else 0
        for k in head[turn:] + head[:turn] + tail:
            part = halve(part, *stages[k], k)
        parts.append(part)
    value = jnp.concatenate(parts, axis=-2) if len(parts) > 1 else parts[0]
    return value.reshape(1, rows, lanes)


def triangle_kernel(block_len, dense, slot_ref, side_ref, w_ref, grad_ref, m_ref, out_ref, send_ref, sym_ref, rest_ref, g_ref, buf_ref):
    test, width = w_ref.shape[1], m_ref.shape[1]
    cells = grad_ref.shape[2]
    for a in range(3):
        for b in range(3):
            g_ref[a, :, pl.ds(b * cells, cells)] = grad_ref[a, b].T
    group = 32
    full = block_len // 128 if dense else out_ref.shape[2] // 128
    out_ref[...] = jnp.zeros(out_ref.shape, out_ref.dtype)
    rest_ref[...] = jnp.zeros(rest_ref.shape, rest_ref.dtype)
    buf_ref[...] = jnp.zeros(buf_ref.shape, buf_ref.dtype)
    if not dense:
        send_ref[...] = jnp.zeros(send_ref.shape, send_ref.dtype)

    def contract(step, carry):
        slabs = []
        for u in range(group):
            i = step * group + u
            zt = w_ref[0, pl.ds(i, 1), :] * g_ref[0]
            zt = zt + w_ref[1, pl.ds(i, 1), :] * g_ref[1]
            zt = zt + w_ref[2, pl.ds(i, 1), :] * g_ref[2]
            slabs.append(zt)
        zt = jnp.concatenate(slabs, axis=0)
        part = jnp.dot(zt, m_ref[...], precision=lax.Precision.HIGH, preferred_element_type=jnp.float32)
        for u in range(group):
            piece = part[u * width : (u + 1) * width, :]
            start = pl.multiple_of((step * group + u) * width, width)
            sym_ref[pl.ds(start, width), :] = piece + piece.T
        return carry

    lax.fori_loop(0, test // group, contract, 0)
    lane = lax.broadcasted_iota(jnp.int32, (test, 128), 1)
    for j in range(width):
        slab = sym_ref[pl.ds(j, test, stride=width), :]
        offset = j * width - (j * (j - 1)) // 2
        stop = offset + width - j
        for c in range(offset // block_len, (stop - 1) // block_len + 1):
            lo = max(offset, c * block_len) - c * block_len
            hi = min(stop, (c + 1) * block_len) - c * block_len
            slot = slot_ref[c]
            for u in range(lo // 128, (hi - 1) // 128 + 1):
                base = c * block_len + u * 128
                rolled = pltpu.roll(slab, (offset - j - base) % 128, 1)
                keep = (lane >= lo - u * 128) & (lane < hi - u * 128)
                if u < full and dense:
                    target = buf_ref.at[(slot + side_ref[0]) % 2, slot // 2, pl.ds(u * test, test), :]
                elif u < full:
                    target = out_ref.at[slot, :, pl.ds(u * 128, 128)]
                else:
                    target = rest_ref.at[slot]
                target[...] = jnp.where(keep, rolled, target[...])
    if dense:
        spare = block_len - full * 128
        row = lax.broadcasted_iota(jnp.int32, (test, 128), 0)
        for s in range(rest_ref.shape[0]):
            tail = rest_ref[s]
            picked = jnp.zeros((test, 128), jnp.float32)
            for r in range(spare):
                hit = (lane >= r * test) & (lane < (r + 1) * test) & (lane - r * test == row)
                picked = jnp.where(hit, jnp.broadcast_to(tail[:, r : r + 1], (test, 128)), picked)
            buf_ref[(s + side_ref[0]) % 2, s // 2, pl.ds(full * test, 1), :] = jnp.sum(picked, axis=0, keepdims=True)
        out_ref[...] = buf_ref[0]
        send_ref[...] = buf_ref[1]


def triangle(slots, side, weighted, grads, modes_flat, block_len, dense):
    owners = slots.shape[0]
    test, width = weighted.shape[1], modes_flat.shape[1]
    tiles = -(-block_len // 128)
    if dense:
        shape = (owners // 2, (block_len // 128) * test + 1, 128)
        spare = (2,) + shape
    else:
        shape = (owners, test, tiles * 128)
        spare = (1, 1, 8, 128)
    return pl.pallas_call(
        functools.partial(triangle_kernel, block_len, dense),
        out_shape=(jax.ShapeDtypeStruct(shape, jnp.float32), jax.ShapeDtypeStruct(shape if dense else (8, 128), jnp.float32)),
        in_specs=[pl.BlockSpec(memory_space=pltpu.SMEM)] * 2 + [pl.BlockSpec(memory_space=pltpu.VMEM)] * 3,
        out_specs=(pl.BlockSpec(memory_space=pltpu.VMEM), pl.BlockSpec(memory_space=pltpu.VMEM)),
        scratch_shapes=[
            pltpu.VMEM((test * width, width), jnp.float32),
            pltpu.VMEM((owners if dense else 1, test, 128), jnp.float32),
            pltpu.VMEM((3, width, 3 * grads.shape[2]), jnp.float32),
            pltpu.VMEM(spare, jnp.float32),
        ],
    )(slots, side, weighted, grads, modes_flat)


def shards(modes, cell_weight, pair_owner):
    width = modes.shape[4]
    size_x = lax.axis_size("gx")
    size_y = lax.axis_size("gy")
    size_z = lax.axis_size("gz")
    owners = size_x * size_y * size_z
    grads = face_gradients(modes)
    mode_flat = modes.reshape(3, -1, width)
    grad_flat = grads.reshape(3, 3, -1, width)
    weight_flat = cell_weight.reshape(-1)
    total_cells = modes.shape[1] * modes.shape[2] * modes.shape[3] * owners
    scale = 1.0 / jnp.sqrt(jnp.float32(3.0 * total_cells))
    cells = mode_flat.shape[1]
    weighted = mode_flat[:, :, :TEST] * (weight_flat * scale)[None, :, None]
    weighted = jnp.tile(jnp.swapaxes(weighted, 1, 2), (1, 1, 3))
    pair_total = width * (width + 1) // 2
    block_len = (pair_total + owners - 1) // owners
    ranks = jnp.arange(owners, dtype=jnp.int32)
    slots = jnp.sum(jnp.where(pair_owner[None, :] == ranks[:, None], ranks[None, :], 0), axis=1)
    slots = jnp.clip(slots, 0, owners - 1).astype(jnp.int32)
    full, spare = block_len // 128, block_len % 128
    dense = 0 < spare and spare * TEST <= 128 and size_z == 2
    side = lax.axis_index("gz").astype(jnp.int32).reshape(1)
    placed, sent = triangle(slots, side, weighted, grad_flat, mode_flat.reshape(3 * cells, width), block_len, dense)
    if dense:
        merged = placed + lax.ppermute(sent, "gz", [(0, 1), (1, 0)])
        owned = scatter_sum(merged, ("gx", "gy"), local=False)[0]
        main = owned[: full * TEST].reshape(full, TEST, 128).transpose(1, 0, 2).reshape(TEST, full * 128)
        tail = owned[full * TEST, : spare * TEST].reshape(spare, TEST).T
        return jnp.concatenate([main, tail], axis=1)
    partial_terms = placed[:, :, :block_len].reshape(owners, TEST * block_len)
    lanes = 128
    rows = -(-TEST * block_len // lanes)
    partial_terms = jnp.pad(partial_terms, ((0, 0), (0, rows * lanes - TEST * block_len)))
    owned = scatter_sum(partial_terms.reshape(owners, rows, lanes), ("gx", "gy", "gz"))
    return owned.reshape(-1)[: TEST * block_len].reshape(TEST, block_len)

def solution(mesh):
    placed = (P("groups", "gx", "gy", "gz", None), P("gx", "gy", "gz"), P())
    return jax.shard_map(
        shards,
        mesh=mesh,
        in_specs=placed,
        out_specs=P("groups", ("gx", "gy", "gz")),
        check_vma=False,
    )
```

```python
import functools

import jax
import jax.numpy as jnp
import numpy as np
from jax import lax
from jax.experimental import pallas as pl
from jax.experimental.pallas import tpu as pltpu
from jax.sharding import PartitionSpec as P

TEST = 64


def extended(value, sides, width):
    for axis, dim in sides:
        peers, length = (lax.axis_size(axis), value.shape[dim])
        up = [(i, (i + 1) % peers) for i in range(peers)]
        down = [(j, i) for i, j in up]
        last = lax.slice_in_dim(value, length - width, length, axis=dim)
        leading = lax.slice_in_dim(value, 0, width, axis=dim)
        before = lax.ppermute(last, axis, up)
        after = lax.ppermute(leading, axis, down)
        value = jnp.concatenate([before, value, after], axis=dim)
    return value


def gradients(padded):
    step_x = (padded[:, 2:, 1:-1, 1:-1] - padded[:, :-2, 1:-1, 1:-1]) * 0.5
    step_y = (padded[:, 1:-1, 2:, 1:-1] - padded[:, 1:-1, :-2, 1:-1]) * 0.5
    step_z = (padded[:, 1:-1, 1:-1, 2:] - padded[:, 1:-1, 1:-1, :-2]) * 0.5
    return jnp.stack([step_x, step_y, step_z], axis=1)


def face_gradients(value):
    steps = []
    for axis, dim in (("gx", 1), ("gy", 2), ("gz", 3)):
        peers, length = lax.axis_size(axis), value.shape[dim]
        up = [(i, (i + 1) % peers) for i in range(peers)]
        down = [(j, i) for i, j in up]
        last = lax.slice_in_dim(value, length - 1, length, axis=dim)
        leading = lax.slice_in_dim(value, 0, 1, axis=dim)
        if axis == "gz" and peers == 2:
            level = lax.axis_index(axis)
            got = lax.ppermute(jnp.where(level == 0, last, leading), axis, [(0, 1), (1, 0)])
            before = jnp.where(level == 1, got, jnp.float32(0.0))
            after = jnp.where(level == 0, got, jnp.float32(0.0))
        else:
            before = lax.ppermute(last, axis, up)
            after = lax.ppermute(leading, axis, down)
            if axis == "gz":
                level = lax.axis_index(axis)
                before = jnp.where(level == 0, jnp.float32(0.0), before)
                after = jnp.where(level == peers - 1, jnp.float32(0.0), after)
        ext = jnp.concatenate([before, value, after], axis=dim)
        high = lax.slice_in_dim(ext, 2, length + 2, axis=dim)
        low = lax.slice_in_dim(ext, 0, length, axis=dim)
        steps.append((high - low) * 0.5)
    return jnp.stack(steps, axis=1)


def halving_stages(axes):
    stages = []
    for axis in axes:
        size = lax.axis_size(axis)
        bit = size // 2
        while bit >= 1:
            stages.append((axis, bit, size))
            bit //= 2
    return stages


def halve(value, axis, bit, size, dim):
    pairs = [(i, i ^ bit) for i in range(size)]
    mine = (lax.axis_index(axis) // bit) % 2
    keep = lax.dynamic_index_in_dim(value, mine, dim, keepdims=True)
    other = lax.dynamic_index_in_dim(value, 1 - mine, dim, keepdims=True)
    return keep + lax.ppermute(other, axis, pairs)


def scatter_sum(payload, axes, local=True):
    sizes = [lax.axis_size(a) for a in axes]
    if any(s & (s - 1) for s in sizes):
        return lax.psum_scatter(payload, tuple(axes), scatter_dimension=0, tiled=True)
    stages = halving_stages(axes)
    rows, lanes = payload.shape[1], payload.shape[2]
    value = payload.reshape((2,) * len(stages) + (rows, lanes))
    first = [k for k, s in enumerate(stages) if local and s[0] == axes[-1]]
    for k in first:
        value = halve(value, *stages[k], k)
    rest = [k for k in range(len(stages)) if k not in first]
    tail = rest[:1] if rest and stages[rest[0]][1] > 1 else []
    head = [k for k in rest if k not in tail][::-1]
    count = min(3, len(rest), rows)
    cuts = np.array_split(np.arange(rows), count) if count else [np.arange(rows)]
    parts = []
    for p, cut in enumerate(cuts):
        part = value[..., int(cut[0]) : int(cut[-1]) + 1, :]
        turn = p % len(head) if head else 0
        for k in head[turn:] + head[:turn] + tail:
            part = halve(part, *stages[k], k)
        parts.append(part)
    value = jnp.concatenate(parts, axis=-2) if len(parts) > 1 else parts[0]
    return value.reshape(1, rows, lanes)


def triangle_kernel(block_len, dense, slot_ref, side_ref, w_ref, grad_ref, m_ref, out_ref, send_ref, sym_ref, rest_ref, g_ref, buf_ref):
    test, width = w_ref.shape[1], m_ref.shape[1]
    cells = grad_ref.shape[2]
    for a in range(3):
        for b in range(3):
            g_ref[a, :, pl.ds(b * cells, cells)] = grad_ref[a, b].T
    group = 32
    full = block_len // 128 if dense else out_ref.shape[2] // 128
    rest_ref[...] = jnp.zeros(rest_ref.shape, rest_ref.dtype)
    buf_ref[...] = jnp.zeros(buf_ref.shape, buf_ref.dtype)
    if not dense:
        out_ref[...] = jnp.zeros(out_ref.shape, out_ref.dtype)
        send_ref[...] = jnp.zeros(send_ref.shape, send_ref.dtype)

    def contract(step, carry):
        slabs = []
        for u in range(group):
            i = step * group + u
            zt = w_ref[0, pl.ds(i, 1), :] * g_ref[0]
            zt = zt + w_ref[1, pl.ds(i, 1), :] * g_ref[1]
            zt = zt + w_ref[2, pl.ds(i, 1), :] * g_ref[2]
            slabs.append(zt)
        zt = jnp.concatenate(slabs, axis=0)
        part = jnp.dot(zt, m_ref[...], precision=lax.Precision.HIGH, preferred_element_type=jnp.float32)
        for u in range(group):
            piece = part[u * width : (u + 1) * width, :]
            start = pl.multiple_of((step * group + u) * width, width)
            sym_ref[pl.ds(start, width), :] = piece + piece.T
        return carry

    lax.fori_loop(0, test // group, contract, 0)
    lane = lax.broadcasted_iota(jnp.int32, (test, 128), 1)
    for j in range(width):
        slab = sym_ref[pl.ds(j, test, stride=width), :]
        offset = j * width - (j * (j - 1)) // 2
        stop = offset + width - j
        for c in range(offset // block_len, (stop - 1) // block_len + 1):
            lo = max(offset, c * block_len) - c * block_len
            hi = min(stop, (c + 1) * block_len) - c * block_len
            slot = slot_ref[c]
            for u in range(lo // 128, (hi - 1) // 128 + 1):
                base = c * block_len + u * 128
                rolled = pltpu.roll(slab, (offset - j - base) % 128, 1)
                keep = (lane >= lo - u * 128) & (lane < hi - u * 128)
                if u < full and dense:
                    target = buf_ref.at[(slot + side_ref[0]) % 2, slot // 2, pl.ds(u * test, test), :]
                elif u < full:
                    target = out_ref.at[slot, :, pl.ds(u * 128, 128)]
                else:
                    target = rest_ref.at[slot]
                target[...] = jnp.where(keep, rolled, target[...])
    if dense:
        spare = block_len - full * 128
        row = lax.broadcasted_iota(jnp.int32, (test, 128), 0)
        for s in range(rest_ref.shape[0]):
            tail = rest_ref[s]
            picked = jnp.zeros((test, 128), jnp.float32)
            for r in range(spare):
                hit = (lane >= r * test) & (lane < (r + 1) * test) & (lane - r * test == row)
                picked = jnp.where(hit, jnp.broadcast_to(tail[:, r : r + 1], (test, 128)), picked)
            buf_ref[(s + side_ref[0]) % 2, s // 2, pl.ds(full * test, 1), :] = jnp.sum(picked, axis=0, keepdims=True)
        out_ref[...] = buf_ref[0]
        send_ref[...] = buf_ref[1]


def triangle(slots, side, weighted, grads, modes_flat, block_len, dense):
    owners = slots.shape[0]
    test, width = weighted.shape[1], modes_flat.shape[1]
    tiles = -(-block_len // 128)
    if dense:
        shape = (owners // 2, (block_len // 128) * test + 1, 128)
        spare = (2,) + shape
    else:
        shape = (owners, test, tiles * 128)
        spare = (1, 1, 8, 128)
    return pl.pallas_call(
        functools.partial(triangle_kernel, block_len, dense),
        out_shape=(jax.ShapeDtypeStruct(shape, jnp.float32), jax.ShapeDtypeStruct(shape if dense else (8, 128), jnp.float32)),
        in_specs=[pl.BlockSpec(memory_space=pltpu.SMEM)] * 2 + [pl.BlockSpec(memory_space=pltpu.VMEM)] * 3,
        out_specs=(pl.BlockSpec(memory_space=pltpu.VMEM), pl.BlockSpec(memory_space=pltpu.VMEM)),
        scratch_shapes=[
            pltpu.VMEM((test * width, width), jnp.float32),
            pltpu.VMEM((owners if dense else 1, test, 128), jnp.float32),
            pltpu.VMEM((3, width, 3 * grads.shape[2]), jnp.float32),
            pltpu.VMEM(spare, jnp.float32),
        ],
    )(slots, side, weighted, grads, modes_flat)


def shards(modes, cell_weight, pair_owner):
    width = modes.shape[4]
    size_x = lax.axis_size("gx")
    size_y = lax.axis_size("gy")
    size_z = lax.axis_size("gz")
    owners = size_x * size_y * size_z
    grads = face_gradients(modes)
    mode_flat = modes.reshape(3, -1, width)
    grad_flat = grads.reshape(3, 3, -1, width)
    weight_flat = cell_weight.reshape(-1)
    total_cells = modes.shape[1] * modes.shape[2] * modes.shape[3] * owners
    scale = 1.0 / jnp.sqrt(jnp.float32(3.0 * total_cells))
    cells = mode_flat.shape[1]
    weighted = mode_flat[:, :, :TEST] * (weight_flat * scale)[None, :, None]
    weighted = jnp.tile(jnp.swapaxes(weighted, 1, 2), (1, 1, 3))
    pair_total = width * (width + 1) // 2
    block_len = (pair_total + owners - 1) // owners
    ranks = jnp.arange(owners, dtype=jnp.int32)
    slots = jnp.sum(jnp.where(pair_owner[None, :] == ranks[:, None], ranks[None, :], 0), axis=1)
    slots = jnp.clip(slots, 0, owners - 1).astype(jnp.int32)
    full, spare = block_len // 128, block_len % 128
    dense = 0 < spare and spare * TEST <= 128 and size_z == 2
    side = lax.axis_index("gz").astype(jnp.int32).reshape(1)
    placed, sent = triangle(slots, side, weighted, grad_flat, mode_flat.reshape(3 * cells, width), block_len, dense)
    if dense:
        merged = placed + lax.ppermute(sent, "gz", [(0, 1), (1, 0)])
        owned = scatter_sum(merged, ("gx", "gy"), local=False)[0]
        main = owned[: full * TEST].reshape(full, TEST, 128).transpose(1, 0, 2).reshape(TEST, full * 128)
        tail = owned[full * TEST, : spare * TEST].reshape(spare, TEST).T
        return jnp.concatenate([main, tail], axis=1)
    partial_terms = placed[:, :, :block_len].reshape(owners, TEST * block_len)
    lanes = 128
    rows = -(-TEST * block_len // lanes)
    partial_terms = jnp.pad(partial_terms, ((0, 0), (0, rows * lanes - TEST * block_len)))
    owned = scatter_sum(partial_terms.reshape(owners, rows, lanes), ("gx", "gy", "gz"))
    return owned.reshape(-1)[: TEST * block_len].reshape(TEST, block_len)

def solution(mesh):
    placed = (P("groups", "gx", "gy", "gz", None), P("gx", "gy", "gz"), P())
    return jax.shard_map(
        shards,
        mesh=mesh,
        in_specs=placed,
        out_specs=P("groups", ("gx", "gy", "gz")),
        check_vma=False,
    )
```
